32 devices in a mesh: ctx: 4 (over z), row: 8 (over y, x, core).
Axes of the slice: x: 2, y: 2, z: 4, core: 2. Of those that a mesh axis runs over, the one named last changes fastest.
Arguments:
- queries: bfloat16 [2048, 2048], P('row'), may hold values from -120 to 120
- keys: bfloat16 [1536, 2048], P('ctx'), may hold values from -5 to 5
- values: bfloat16 [1536, 2048], P('ctx'), may hold values from -6 to 6
- block_list: int32 [16, 8], P('row'), may hold values from 0 to 11, as said below
- block_count: int32 [16], P('row'), may hold values from 1 to 8, as said below
Outputs:
- owned: bfloat16 [2048, 2048], P('row', 'ctx')
The draws below stay inside these ranges and needn't reach their ends.
Inputs may be any that keep to these rules, and one draw needn't show every extreme that they name: `block_list`: entries of one list are distinct; the first entry of the list of query block b is b % 12. Entries past block_count are ignored. `block_count`: every query block uses at least one list entry.
All inputs are finite; a program needn't handle non-finite values.
Results may differ from the reference program's by a relative error of at most 0.0044.
Values may be sent and summed in bfloat16 or wider, within the bound.
No kernel may reach another device: no remote copies, remote signals or barrier semaphores. Data moves between devices by JAX's collectives and lax.ppermute only.
A program may use at most 64 MiB of HBM per device.

```python
import jax
import jax.numpy as jnp
from jax import lax

HEADS = 16
HEAD_DIM = 128
BLOCK = 128
MAXSEL = 8
Q_DEV = 256
KB_DEV = 3
WIDTH = 2048
CTX_DEV = 384
KBLOCKS = 12
CTXLEN = 1536
QROWS = 2048
QBLOCKS = 16
N_CTX = 4
N_ROW = 8


def shared_keys(key):
    normal_keys = jnp.clip(jax.random.normal(jax.random.fold_in(key, 7), (CTXLEN, WIDTH), jnp.float32), -5.0, 5.0)
    return normal_keys


def draw_keys(key, part):
    return shared_keys(key).astype(jnp.bfloat16)


def draw_queries(key, part):
    base_draw = jnp.clip(jax.random.normal(jax.random.fold_in(key, 3), (QROWS, WIDTH), jnp.float32), -5.0, 5.0)
    return base_draw.astype(jnp.bfloat16)


def draw_block_list(key, part):
    raw_scores = jax.random.randint(jax.random.fold_in(key, 5), (QBLOCKS, KBLOCKS - 1), 0, 2 ** 20)
    distinct = raw_scores * KBLOCKS + jnp.arange(KBLOCKS - 1, dtype=jnp.int32)[None, :]
    order = jnp.argsort(distinct, axis=1, stable=True).astype(jnp.int32)
    offsets = jnp.concatenate([jnp.zeros((QBLOCKS, 1), jnp.int32), order + 1], axis=1)[:, :MAXSEL]
    anchors = jnp.arange(QBLOCKS, dtype=jnp.int32) % KBLOCKS
    return (anchors[:, None] + offsets) % KBLOCKS


def draw_block_count(key, part):
    counts = jax.random.randint(jax.random.fold_in(key, 9), (QBLOCKS,), 1, MAXSEL + 1)
    return counts.at[0].set(MAXSEL).at[1].set(1)


def levels(rng, extent, cuts, smallest, high):
    gain = 1.0
    for axis_at, shards_of in cuts:
        draws = jax.random.uniform(jax.random.fold_in(jax.random.fold_in(rng, 6), axis_at), (shards_of,), jnp.float32, smallest / len(cuts), high / len(cuts))
        gain = gain * jnp.repeat(jnp.exp(draws), extent[axis_at] // shards_of).reshape((-1,) + (1,) * (len(extent) - 1 - axis_at))
    return gain


def scatter_about(key, extent, width, limit, pieces=(), kind=jnp.bfloat16):
    entries = jax.random.normal(key, extent, jnp.float32) * width
    if len(pieces) > 0:
        entries = levels(key, extent, pieces, -0.22, 0.18) * entries
    return jnp.clip(entries, min=-limit, max=limit).astype(kind)


def setup_inputs(seed: int = 0) -> dict:
    key_of = jax.random.split(jax.random.key(seed), 6)
    return {
        "queries": draw_queries(jax.random.fold_in(key_of[5], 71), 0),
        "keys": draw_keys(jax.random.fold_in(key_of[5], 71), 0),
        "values": scatter_about(key_of[2], (CTXLEN, WIDTH), 1.0, 6.0, ((0, 4),)),
        "block_list": draw_block_list(jax.random.fold_in(key_of[5], 71), 0),
        "block_count": draw_block_count(jax.random.fold_in(key_of[5], 71), 0),
    }


masked_fill = -1e30


def selected_blocks(block_list, block_count):
    slot_live = jnp.arange(block_list.shape[1], dtype=jnp.int32)[None, :] < block_count[:, None]
    block_ids = jnp.arange(KBLOCKS, dtype=jnp.int32)
    block_hits = (block_list[:, :, None] == block_ids[None, None, :]) & slot_live[:, :, None]
    return jnp.any(block_hits, axis=1)


def reference(queries, keys, values, block_list, block_count):
    chosen = selected_blocks(block_list, block_count)
    row_chosen = jnp.repeat(chosen, BLOCK, axis=0)
    query_float = queries.astype(jnp.float32).reshape(QROWS, HEADS, HEAD_DIM)
    score_scale = 1.0 / (HEAD_DIM ** 0.5)

    def segment_step(state_now, segment):
        best_now, total_now, numer_now = state_now
        start = (segment * CTX_DEV).astype(jnp.int32)
        key_block = lax.dynamic_slice_in_dim(keys, start, CTX_DEV, 0).astype(jnp.float32).reshape(CTX_DEV, HEADS, HEAD_DIM)
        value_block = lax.dynamic_slice_in_dim(values, start, CTX_DEV, 0).astype(jnp.float32).reshape(CTX_DEV, HEADS, HEAD_DIM)
        mask_block = lax.dynamic_slice_in_dim(row_chosen, (segment * KB_DEV).astype(jnp.int32), KB_DEV, 1)
        mask_block = jnp.repeat(mask_block, BLOCK, axis=1)[None, :, :]
        scores = jnp.einsum('qhd,khd->hqk', query_float, key_block) * score_scale
        seg_max = jnp.max(jnp.where(mask_block, scores, masked_fill), axis=2)
        probs_live = jnp.where(mask_block, jnp.exp(scores - seg_max[:, :, None]), 0.0)
        seg_total = jnp.sum(probs_live, axis=2)
        probs_low = probs_live.astype(jnp.bfloat16).astype(jnp.float32)
        seg_out = jnp.einsum('hqk,khd->hqd', probs_low, value_block)
        best_new = jnp.maximum(best_now, seg_max)
        old_weight = jnp.exp(best_now - best_new)
        seg_weight = jnp.exp(seg_max - best_new)
        total_new = total_now * old_weight + seg_total * seg_weight
        numer_new = numer_now * old_weight[:, :, None] + seg_out * seg_weight[:, :, None]
        return (best_new, total_new, numer_new), None

    start_state = (jnp.full((HEADS, QROWS), masked_fill, jnp.float32),
                   jnp.zeros((HEADS, QROWS), jnp.float32),
                   jnp.zeros((HEADS, QROWS, HEAD_DIM), jnp.float32))
    final_state, unused = lax.scan(segment_step, start_state, jnp.arange(N_CTX, dtype=jnp.int32))
    best_all, total_all, numer_all = final_state
    attended = numer_all / total_all[:, :, None]
    attended = jnp.transpose(attended, (1, 0, 2)).reshape(QROWS, WIDTH).astype(jnp.bfloat16)
    owned = jnp.transpose(attended.reshape(Q_DEV, N_ROW, WIDTH), (1, 0, 2)).reshape(QROWS, WIDTH)
    return owned
```

```python
import jax
import jax.numpy as jnp
from jax import lax
from jax.sharding import PartitionSpec as P

HEADS = 16
HEAD_DIM = 128
BLOCK = 128


masked_fill = -1e30


def chosen_range(block_list, block_count, first_block, block_span):
    slot_live = jnp.arange(block_list.shape[1], dtype=jnp.int32)[None, :] < block_count[:, None]
    block_ids = first_block + jnp.arange(block_span, dtype=jnp.int32)
    block_hits = (block_list[:, :, None] == block_ids[None, None, :]) & slot_live[:, :, None]
    return jnp.any(block_hits, axis=1)


def segment_parts(query_heads, key_heads, value_heads, chosen):
    key_live = jnp.repeat(jnp.repeat(chosen, BLOCK, axis=0), BLOCK, axis=1)[None, :, :]
    score_scale = 1.0 / HEAD_DIM**0.5
    scores = (
        jnp.einsum("qhd,khd->hqk", query_heads, key_heads, preferred_element_type=jnp.float32)
        * score_scale
    )
    seg_max = jnp.max(jnp.where(key_live, scores, masked_fill), axis=2)
    probs_live = jnp.where(key_live, jnp.exp(scores - seg_max[:, :, None]), 0.0)
    seg_total = jnp.sum(probs_live, axis=2)
    probs_low = probs_live.astype(jnp.bfloat16)
    seg_out = jnp.einsum("hqk,khd->hqd", probs_low, value_heads, preferred_element_type=jnp.float32)
    return (seg_max, seg_total, seg_out)


def local(queries, keys, values, block_list, block_count):
    row_count = queries.shape[0]
    ctx_span = keys.shape[0]
    shards = lax.axis_size("ctx")
    head_share = HEADS // shards
    share_width = head_share * HEAD_DIM
    blocks_here = ctx_span // BLOCK
    chosen = chosen_range(block_list, block_count, lax.axis_index("ctx") * blocks_here, blocks_here)
    seg_max, seg_total, seg_out = segment_parts(
        queries.reshape(row_count, HEADS, HEAD_DIM),
        keys.reshape(ctx_span, HEADS, HEAD_DIM),
        values.reshape(ctx_span, HEADS, HEAD_DIM),
        chosen,
    )
    stats = jnp.stack(
        [seg_max.reshape(shards, head_share, row_count), seg_total.reshape(shards, head_share, row_count)],
        axis=1,
    )
    part_low = seg_out.astype(jnp.bfloat16).reshape(shards, head_share, row_count, HEAD_DIM)
    stats_in = lax.all_to_all(stats, "ctx", 0, 0, tiled=True)
    part_in = lax.all_to_all(part_low, "ctx", 0, 0, tiled=True)
    maxima = stats_in[:, 0]
    totals = stats_in[:, 1]
    row_best = jnp.max(maxima, axis=0)
    weight = jnp.exp(maxima - row_best[None])
    total_sum = jnp.sum(totals * weight, axis=0)
    numerator = jnp.sum(part_in.astype(jnp.float32) * weight[:, :, :, None], axis=0)
    attended = numerator / total_sum[:, :, None]
    attended_low = jnp.transpose(attended, (1, 0, 2)).reshape(row_count, share_width).astype(jnp.bfloat16)
    owners = lax.axis_size("row")
    per_owner = row_count // owners
    grouped = jnp.transpose(attended_low.reshape(per_owner, owners, share_width), (1, 0, 2))
    regrouped = lax.all_to_all(grouped, "row", 0, 0, tiled=True)
    return regrouped.reshape(row_count, share_width)


def solution(mesh):
    return jax.shard_map(
        local,
        mesh=mesh,
        in_specs=(P("row", None), P("ctx", None), P("ctx", None), P("row", None), P("row")),
        out_specs=P("row", "ctx"),
        check_vma=False,
    )
```

```python
import jax
import jax.numpy as jnp
from jax import lax
from jax.sharding import PartitionSpec as P

HEADS = 16
HEAD_DIM = 128
BLOCK = 128


masked_fill = -1e30


def chosen_range(block_list, block_count, first_block, block_span):
    slot_live = jnp.arange(block_list.shape[1], dtype=jnp.int32)[None, :] < block_count[:, None]
    block_ids = first_block + jnp.arange(block_span, dtype=jnp.int32)
    block_hits = (block_list[:, :, None] == block_ids[None, None, :]) & slot_live[:, :, None]
    return jnp.any(block_hits, axis=1)


def segment_parts(query_heads, key_heads, value_heads, chosen):
    key_live = jnp.repeat(jnp.repeat(chosen, BLOCK, axis=0), BLOCK, axis=1)[None, :, :]
    score_scale = 1.0 / HEAD_DIM**0.5
    scores = (
        jnp.einsum("qhd,khd->hqk", query_heads, key_heads, preferred_element_type=jnp.float32)
        * score_scale
    )
    seg_max = jnp.max(jnp.where(key_live, scores, masked_fill), axis=2)
    probs_live = jnp.where(key_live, jnp.exp(scores - seg_max[:, :, None]), 0.0)
    seg_total = jnp.sum(probs_live, axis=2)
    probs_low = probs_live.astype(jnp.bfloat16)
    seg_out = jnp.einsum("hqk,khd->hqd", probs_low, value_heads, preferred_element_type=jnp.float32)
    return (seg_max, seg_total, seg_out)


def split_three(x):
    hi = lax.reduce_precision(x, exponent_bits=8, mantissa_bits=7)
    rest = x - hi
    mid = lax.reduce_precision(rest, exponent_bits=8, mantissa_bits=7)
    lo = lax.reduce_precision(rest - mid, exponent_bits=8, mantissa_bits=7)
    return jnp.stack([hi, mid, lo], axis=1).astype(jnp.bfloat16)


def join_three(parts):
    parts = parts.astype(jnp.float32)
    return (parts[:, 0] + parts[:, 1]) + parts[:, 2]


def local(queries, keys, values, block_list, block_count):
    row_count = queries.shape[0]
    ctx_span = keys.shape[0]
    shards = lax.axis_size("ctx")
    head_share = HEADS // shards
    share_width = head_share * HEAD_DIM
    blocks_here = ctx_span // BLOCK
    chosen = chosen_range(block_list, block_count, lax.axis_index("ctx") * blocks_here, blocks_here)
    seg_max, seg_total, seg_out = segment_parts(
        queries.reshape(row_count, HEADS, HEAD_DIM),
        keys.reshape(ctx_span, HEADS, HEAD_DIM),
        values.reshape(ctx_span, HEADS, HEAD_DIM),
        chosen,
    )
    stats = jnp.stack(
        [seg_max.reshape(shards, head_share, row_count), seg_total.reshape(shards, head_share, row_count)],
        axis=1,
    )
    part_low = seg_out.astype(jnp.bfloat16).reshape(shards, head_share * row_count, HEAD_DIM)
    stat_rows = 3 * 2 * head_share * row_count // HEAD_DIM
    payload = jnp.concatenate(
        [part_low, split_three(stats).reshape(shards, stat_rows, HEAD_DIM)], axis=1
    )
    arrived = lax.all_to_all(payload, "ctx", 0, 0, tiled=True)
    part_in = arrived[:, : head_share * row_count].reshape(shards, head_share, row_count, HEAD_DIM)
    stats_in = join_three(arrived[:, head_share * row_count :].reshape(shards, 3, 2, head_share, row_count))
    maxima = stats_in[:, 0]
    totals = stats_in[:, 1]
    row_best = jnp.max(maxima, axis=0)
    weight = jnp.exp(maxima - row_best[None])
    total_sum = jnp.sum(totals * weight, axis=0)
    numerator = jnp.sum(part_in.astype(jnp.float32) * weight[:, :, :, None], axis=0)
    attended = numerator / total_sum[:, :, None]
    attended_low = jnp.transpose(attended, (1, 0, 2)).reshape(row_count, share_width).astype(jnp.bfloat16)
    owners = lax.axis_size("row")
    per_owner = row_count // owners
    grouped = jnp.transpose(attended_low.reshape(per_owner, owners, share_width), (1, 0, 2))
    regrouped = lax.all_to_all(grouped, "row", 0, 0, tiled=True)
    return regrouped.reshape(row_count, share_width)


def solution(mesh):
    return jax.shard_map(
        local,
        mesh=mesh,
        in_specs=(P("row", None), P("ctx", None), P("ctx", None), P("row", None), P("row")),
        out_specs=P("row", "ctx"),
        check_vma=False,
    )
```

```python
import jax
import jax.numpy as jnp
from jax import lax
from jax.sharding import PartitionSpec as P

HEADS = 16
HEAD_DIM = 128
BLOCK = 128


masked_fill = -1e30


def chosen_range(block_list, block_count, first_block, block_span):
    slot_live = jnp.arange(block_list.shape[1], dtype=jnp.int32)[None, :] < block_count[:, None]
    block_ids = first_block + jnp.arange(block_span, dtype=jnp.int32)
    block_hits = (block_list[:, :, None] == block_ids[None, None, :]) & slot_live[:, :, None]
    return jnp.any(block_hits, axis=1)


def segment_parts(query_heads, key_heads, value_heads, chosen):
    key_live = jnp.repeat(jnp.repeat(chosen, BLOCK, axis=0), BLOCK, axis=1)[None, :, :]
    score_scale = 1.0 / HEAD_DIM**0.5
    scores = (
        jnp.einsum("qhd,khd->hqk", query_heads, key_heads, preferred_element_type=jnp.float32)
        * score_scale
    )
    seg_max = jnp.max(jnp.where(key_live, scores, masked_fill), axis=2)
    probs_live = jnp.where(key_live, jnp.exp(scores - seg_max[:, :, None]), 0.0)
    seg_total = jnp.sum(probs_live, axis=2)
    probs_low = probs_live.astype(jnp.bfloat16)
    seg_out = jnp.einsum("hqk,khd->hqd", probs_low, value_heads, preferred_element_type=jnp.float32)
    return (seg_max, seg_total, seg_out)


def split_three(x):
    hi = lax.reduce_precision(x, exponent_bits=8, mantissa_bits=7)
    rest = x - hi
    mid = lax.reduce_precision(rest, exponent_bits=8, mantissa_bits=7)
    lo = lax.reduce_precision(rest - mid, exponent_bits=8, mantissa_bits=7)
    return jnp.stack([hi, mid, lo], axis=1).astype(jnp.bfloat16)


def join_three(parts):
    parts = parts.astype(jnp.float32)
    return (parts[:, 0] + parts[:, 1]) + parts[:, 2]


def local(queries, keys, values, block_list, block_count):
    row_count = queries.shape[0]
    ctx_span = keys.shape[0]
    shards = lax.axis_size("ctx")
    head_share = HEADS // shards
    share_width = head_share * HEAD_DIM
    blocks_here = ctx_span // BLOCK
    chosen = chosen_range(block_list, block_count, lax.axis_index("ctx") * blocks_here, blocks_here)
    seg_max, seg_total, seg_out = segment_parts(
        queries.reshape(row_count, HEADS, HEAD_DIM),
        keys.reshape(ctx_span, HEADS, HEAD_DIM),
        values.reshape(ctx_span, HEADS, HEAD_DIM),
        chosen,
    )
    owners = lax.axis_size("row")
    per_owner = row_count // owners
    part_low = seg_out.astype(jnp.bfloat16).reshape(shards, head_share, per_owner, owners, HEAD_DIM)
    part_low = jnp.transpose(part_low, (3, 0, 1, 2, 4)).reshape(
        owners * shards, head_share * per_owner, HEAD_DIM
    )
    stats = jnp.stack([seg_max, seg_total]).reshape(2, shards, head_share, per_owner, owners)
    stats = jnp.transpose(stats, (4, 1, 0, 2, 3)).reshape(owners * shards, 2, head_share, per_owner)
    stat_count = 3 * 2 * head_share * per_owner
    stat_rows = -(-stat_count // HEAD_DIM)
    stat_low = split_three(stats).reshape(owners * shards, stat_count)
    stat_low = jnp.pad(stat_low, ((0, 0), (0, stat_rows * HEAD_DIM - stat_count)))
    payload = jnp.concatenate(
        [part_low, stat_low.reshape(owners * shards, stat_rows, HEAD_DIM)], axis=1
    )
    arrived = lax.all_to_all(payload, ("row", "ctx"), 0, 0, tiled=True)
    arrived = arrived.reshape(owners, shards, head_share * per_owner + stat_rows, HEAD_DIM)
    part_in = arrived[:, :, : head_share * per_owner].reshape(owners, shards, head_share, per_owner, HEAD_DIM)
    stat_in = arrived[:, :, head_share * per_owner :].reshape(owners * shards, stat_rows * HEAD_DIM)
    stats_in = join_three(
        stat_in[:, :stat_count].reshape(owners * shards, 3, 2, head_share, per_owner)
    ).reshape(owners, shards, 2, head_share, per_owner)
    maxima = stats_in[:, :, 0]
    totals = stats_in[:, :, 1]
    row_best = jnp.max(maxima, axis=1)
    weight = jnp.exp(maxima - row_best[:, None])
    total_sum = jnp.sum(totals * weight, axis=1)
    numerator = jnp.sum(part_in.astype(jnp.float32) * weight[..., None], axis=1)
    attended = numerator / total_sum[..., None]
    attended_low = jnp.transpose(attended, (0, 2, 1, 3)).reshape(row_count, share_width)
    return attended_low.astype(jnp.bfloat16)


def solution(mesh):
    return jax.shard_map(
        local,
        mesh=mesh,
        in_specs=(P("row", None), P("ctx", None), P("ctx", None), P("row", None), P("row")),
        out_specs=P("row", "ctx"),
        check_vma=False,
    )
```

```python
import functools

import jax
import jax.numpy as jnp
from jax import lax
from jax.experimental import pallas as pl
from jax.experimental.pallas import tpu as pltpu
from jax.sharding import PartitionSpec as P

HEADS = 16
HEAD_DIM = 128
BLOCK = 128


masked_fill = -1e30


def attention_kernel(shape, list_ref, count_ref, first_ref, q_ref, k_ref, v_ref, part_ref, stat_ref,
                     bias_ref, any_ref):
    owners, per_owner, head_share, q_blocks, k_blocks, max_sel = shape
    rows = owners * per_owner

    @pl.when(pl.program_id(0) == 0)
    def _():
        first = first_ref[0]
        pos = lax.broadcasted_iota(jnp.int32, (rows, 1), 0)
        frame = (pos % per_owner) * owners + pos // per_owner
        q_block = frame // BLOCK
        any_live = jnp.zeros((rows, 1), jnp.int32)
        for b in range(k_blocks):
            live = jnp.zeros((rows, 1), jnp.int32)
            for a in range(q_blocks):
                hit = jnp.int32(0)
                for slot in range(max_sel):
                    found = (list_ref[a * max_sel + slot] == first + b) & (slot < count_ref[a])
                    hit = jnp.maximum(hit, jnp.where(found, 1, 0).astype(jnp.int32))
                live = jnp.where(q_block == a, hit, live)
            any_live = jnp.maximum(any_live, live)
            bias = jnp.where(live > 0, 0.0, masked_fill).astype(jnp.float32)
            bias_ref[:, b * BLOCK : (b + 1) * BLOCK] = jnp.broadcast_to(bias, (rows, BLOCK))
        any_ref[...] = jnp.broadcast_to(any_live, (rows, HEAD_DIM))

    score_scale = 1.0 / HEAD_DIM**0.5
    row_live = any_ref[:, 0:1] > 0
    for hl in range(head_share):
        cols = slice(hl * HEAD_DIM, (hl + 1) * HEAD_DIM)
        scores = lax.dot_general(
            q_ref[:, cols], k_ref[:, cols], (((1,), (1,)), ((), ())), preferred_element_type=jnp.float32
        )
        scores = scores * score_scale + bias_ref[...]
        seg_max = jnp.max(scores, axis=1, keepdims=True)
        probs = jnp.exp(scores - seg_max)
        seg_total = jnp.where(row_live, jnp.sum(probs, axis=1, keepdims=True), 0.0)
        seg_out = jnp.dot(probs.astype(jnp.bfloat16), v_ref[:, cols], preferred_element_type=jnp.float32)
        seg_out = jnp.where(row_live, seg_out, 0.0)
        part_ref[:, hl, :, :] = seg_out.reshape(owners, per_owner, HEAD_DIM).astype(jnp.bfloat16)
        stat_ref[hl, :, 0:1] = seg_max
        stat_ref[hl, :, 1:2] = seg_total


def local_attention(queries_perm, keys, values, block_list, block_count, first_block, owners, shards):
    rows = queries_perm.shape[0]
    ctx_span = keys.shape[0]
    per_owner = rows // owners
    head_share = HEADS // shards
    share_width = head_share * HEAD_DIM
    q_blocks = rows // BLOCK
    k_blocks = ctx_span // BLOCK
    max_sel = block_list.shape[1]
    shape = (owners, per_owner, head_share, q_blocks, k_blocks, max_sel)
    grid_spec = pltpu.PrefetchScalarGridSpec(
        num_scalar_prefetch=3,
        grid=(shards,),
        in_specs=[
            pl.BlockSpec((rows, share_width), lambda g, *_: (0, g)),
            pl.BlockSpec((ctx_span, share_width), lambda g, *_: (0, g)),
            pl.BlockSpec((ctx_span, share_width), lambda g, *_: (0, g)),
        ],
        out_specs=[
            pl.BlockSpec((owners, head_share, per_owner, HEAD_DIM), lambda g, *_: (0, g, 0, 0)),
            pl.BlockSpec((head_share, rows, 2), lambda g, *_: (g, 0, 0)),
        ],
        scratch_shapes=[
            pltpu.VMEM((rows, ctx_span), jnp.float32),
            pltpu.VMEM((rows, HEAD_DIM), jnp.int32),
        ],
    )
    flops = 4 * HEADS * rows * ctx_span * HEAD_DIM
    return pl.pallas_call(
        functools.partial(attention_kernel, shape),
        grid_spec=grid_spec,
        out_shape=[
            jax.ShapeDtypeStruct((owners, HEADS, per_owner, HEAD_DIM), jnp.bfloat16),
            jax.ShapeDtypeStruct((HEADS, rows, 2), jnp.float32),
        ],
        compiler_params=pltpu.CompilerParams(dimension_semantics=("arbitrary",)),
        cost_estimate=pl.CostEstimate(
            flops=flops,
            transcendentals=HEADS * rows * ctx_span,
            bytes_accessed=2 * (queries_perm.size + keys.size + values.size) + 2 * rows * HEADS * HEAD_DIM,
        ),
    )(block_list.reshape(-1), block_count, first_block, queries_perm, keys, values)


def split_three(x):
    hi = lax.reduce_precision(x, exponent_bits=8, mantissa_bits=7)
    rest = x - hi
    mid = lax.reduce_precision(rest, exponent_bits=8, mantissa_bits=7)
    lo = lax.reduce_precision(rest - mid, exponent_bits=8, mantissa_bits=7)
    return jnp.stack([hi, mid, lo], axis=1).astype(jnp.bfloat16)


def join_three(parts):
    parts = parts.astype(jnp.float32)
    return (parts[:, 0] + parts[:, 1]) + parts[:, 2]


def local(queries, keys, values, block_list, block_count):
    row_count = queries.shape[0]
    ctx_span = keys.shape[0]
    shards = lax.axis_size("ctx")
    owners = lax.axis_size("row")
    per_owner = row_count // owners
    head_share = HEADS // shards
    share_width = head_share * HEAD_DIM
    blocks_here = ctx_span // BLOCK
    first_block = (lax.axis_index("ctx") * blocks_here).astype(jnp.int32).reshape(1)
    queries_perm = jnp.transpose(queries.reshape(per_owner, owners, -1), (1, 0, 2)).reshape(row_count, -1)
    part, stat = local_attention(
        queries_perm, keys, values, block_list, block_count.astype(jnp.int32), first_block, owners, shards
    )
    part_low = part.reshape(owners * shards, head_share * per_owner, HEAD_DIM)
    stats = jnp.transpose(stat.reshape(shards, head_share, owners, per_owner, 2), (2, 0, 4, 1, 3))
    stats = stats.reshape(owners * shards, 2, head_share, per_owner)
    stat_count = 3 * 2 * head_share * per_owner
    stat_rows = -(-stat_count // HEAD_DIM)
    stat_low = split_three(stats).reshape(owners * shards, stat_count)
    stat_low = jnp.pad(stat_low, ((0, 0), (0, stat_rows * HEAD_DIM - stat_count)))
    payload = jnp.concatenate(
        [part_low, stat_low.reshape(owners * shards, stat_rows, HEAD_DIM)], axis=1
    )
    arrived = lax.all_to_all(payload, ("row", "ctx"), 0, 0, tiled=True)
    arrived = arrived.reshape(owners, shards, head_share * per_owner + stat_rows, HEAD_DIM)
    part_in = arrived[:, :, : head_share * per_owner].reshape(owners, shards, head_share, per_owner, HEAD_DIM)
    stat_in = arrived[:, :, head_share * per_owner :].reshape(owners * shards, stat_rows * HEAD_DIM)
    stats_in = join_three(
        stat_in[:, :stat_count].reshape(owners * shards, 3, 2, head_share, per_owner)
    ).reshape(owners, shards, 2, head_share, per_owner)
    maxima = stats_in[:, :, 0]
    totals = stats_in[:, :, 1]
    row_best = jnp.max(maxima, axis=1)
    weight = jnp.exp(maxima - row_best[:, None])
    total_sum = jnp.sum(totals * weight, axis=1)
    numerator = jnp.sum(part_in.astype(jnp.float32) * weight[..., None], axis=1)
    attended = numerator / total_sum[..., None]
    attended_low = jnp.transpose(attended, (0, 2, 1, 3)).reshape(row_count, share_width)
    return attended_low.astype(jnp.bfloat16)


def solution(mesh):
    return jax.shard_map(
        local,
        mesh=mesh,
        in_specs=(P("row", None), P("ctx", None), P("ctx", None), P("row", None), P("row")),
        out_specs=P("row", "ctx"),
        check_vma=False,
    )
```

```python
import functools

import jax
import jax.numpy as jnp
from jax import lax
from jax.experimental import pallas as pl
from jax.experimental.pallas import tpu as pltpu
from jax.sharding import PartitionSpec as P

HEADS = 16
HEAD_DIM = 128
BLOCK = 128


masked_fill = -1e30


def attention_kernel(shape, list_ref, count_ref, first_ref, q_ref, k_ref, v_ref, part_ref, stat_ref,
                     bias_ref, any_ref):
    rows, head_share, q_blocks, k_blocks, max_sel = shape

    @pl.when(pl.program_id(0) == 0)
    def _():
        first = first_ref[0]
        for a in range(q_blocks):
            any_live = jnp.int32(0)
            for b in range(k_blocks):
                hit = jnp.int32(0)
                for slot in range(max_sel):
                    found = (list_ref[a, slot] == first + b) & (slot < count_ref[a])
                    hit = jnp.maximum(hit, jnp.where(found, 1, 0).astype(jnp.int32))
                any_live = jnp.maximum(any_live, hit)
                bias = jnp.where(hit > 0, 0.0, masked_fill).astype(jnp.float32)
                bias_ref[a * BLOCK : (a + 1) * BLOCK, b * BLOCK : (b + 1) * BLOCK] = jnp.full(
                    (BLOCK, BLOCK), bias, jnp.float32
                )
            any_ref[a * BLOCK : (a + 1) * BLOCK, :] = jnp.full((BLOCK, HEAD_DIM), any_live, jnp.int32)

    score_scale = 1.0 / HEAD_DIM**0.5
    row_live = any_ref[:, 0:1] > 0
    lane = lax.broadcasted_iota(jnp.int32, (rows, HEAD_DIM), 1)
    stats = jnp.zeros((rows, HEAD_DIM), jnp.float32)
    for hl in range(head_share):
        cols = slice(hl * HEAD_DIM, (hl + 1) * HEAD_DIM)
        scores = lax.dot_general(
            q_ref[:, cols], k_ref[:, cols], (((1,), (1,)), ((), ())), preferred_element_type=jnp.float32
        )
        scores = scores * score_scale + bias_ref[...]
        seg_max = jnp.max(scores, axis=1, keepdims=True)
        probs = jnp.exp(scores - seg_max)
        seg_total = jnp.where(row_live, jnp.sum(probs, axis=1, keepdims=True), 0.0)
        seg_out = jnp.dot(probs.astype(jnp.bfloat16), v_ref[:, cols], preferred_element_type=jnp.float32)
        part_ref[hl] = jnp.where(row_live, seg_out, 0.0).astype(jnp.bfloat16)
        stats = jnp.where(lane == hl, seg_max, stats)
        stats = jnp.where(lane == head_share + hl, seg_total, stats)
    stat_ref[0] = jnp.transpose(stats)[: 2 * head_share]


def local_attention(queries, keys, values, block_list, block_count, first_block, shards):
    rows = queries.shape[0]
    ctx_span = keys.shape[0]
    head_share = HEADS // shards
    share_width = head_share * HEAD_DIM
    q_blocks = rows // BLOCK
    k_blocks = ctx_span // BLOCK
    max_sel = block_list.shape[1]
    shape = (rows, head_share, q_blocks, k_blocks, max_sel)
    grid_spec = pltpu.PrefetchScalarGridSpec(
        num_scalar_prefetch=3,
        grid=(shards,),
        in_specs=[
            pl.BlockSpec((rows, share_width), lambda g, *_: (0, g)),
            pl.BlockSpec((ctx_span, share_width), lambda g, *_: (0, g)),
            pl.BlockSpec((ctx_span, share_width), lambda g, *_: (0, g)),
        ],
        out_specs=[
            pl.BlockSpec((head_share, rows, HEAD_DIM), lambda g, *_: (g, 0, 0)),
            pl.BlockSpec((1, 2 * head_share, rows), lambda g, *_: (g, 0, 0)),
        ],
        scratch_shapes=[
            pltpu.VMEM((rows, ctx_span), jnp.float32),
            pltpu.VMEM((rows, HEAD_DIM), jnp.int32),
        ],
    )
    flops = 4 * HEADS * rows * ctx_span * HEAD_DIM
    return pl.pallas_call(
        functools.partial(attention_kernel, shape),
        grid_spec=grid_spec,
        out_shape=[
            jax.ShapeDtypeStruct((HEADS, rows, HEAD_DIM), jnp.bfloat16),
            jax.ShapeDtypeStruct((shards, 2 * head_share, rows), jnp.float32),
        ],
        compiler_params=pltpu.CompilerParams(dimension_semantics=("arbitrary",)),
        cost_estimate=pl.CostEstimate(
            flops=flops,
            transcendentals=HEADS * rows * ctx_span,
            bytes_accessed=2 * (queries.size + keys.size + values.size) + 2 * rows * HEADS * HEAD_DIM,
        ),
    )(block_list, block_count, first_block, queries, keys, values)


def split_three(x):
    hi = lax.reduce_precision(x, exponent_bits=8, mantissa_bits=7)
    rest = x - hi
    mid = lax.reduce_precision(rest, exponent_bits=8, mantissa_bits=7)
    lo = lax.reduce_precision(rest - mid, exponent_bits=8, mantissa_bits=7)
    return jnp.stack([hi, mid, lo], axis=1).astype(jnp.bfloat16)


def join_three(parts):
    parts = parts.astype(jnp.float32)
    return (parts[:, 0] + parts[:, 1]) + parts[:, 2]


def local(queries, keys, values, block_list, block_count):
    row_count = queries.shape[0]
    ctx_span = keys.shape[0]
    shards = lax.axis_size("ctx")
    owners = lax.axis_size("row")
    per_owner = row_count // owners
    head_share = HEADS // shards
    share_width = head_share * HEAD_DIM
    blocks_here = ctx_span // BLOCK
    first_block = (lax.axis_index("ctx") * blocks_here).astype(jnp.int32).reshape(1)
    part, stat = local_attention(
        queries, keys, values, block_list.astype(jnp.int32), block_count.astype(jnp.int32), first_block, shards
    )
    part_low = part.reshape(shards, head_share, per_owner, owners, HEAD_DIM)
    part_low = jnp.transpose(part_low, (3, 0, 1, 2, 4)).reshape(
        owners * shards, head_share * per_owner, HEAD_DIM
    )
    stats = jnp.transpose(stat.reshape(shards, 2, head_share, per_owner, owners), (4, 0, 1, 2, 3))
    stats = stats.reshape(owners * shards, 2, head_share, per_owner)
    stat_count = 3 * 2 * head_share * per_owner
    stat_rows = -(-stat_count // HEAD_DIM)
    stat_low = split_three(stats).reshape(owners * shards, stat_count)
    stat_low = jnp.pad(stat_low, ((0, 0), (0, stat_rows * HEAD_DIM - stat_count)))
    payload = jnp.concatenate(
        [part_low, stat_low.reshape(owners * shards, stat_rows, HEAD_DIM)], axis=1
    )
    arrived = lax.all_to_all(payload, ("row", "ctx"), 0, 0, tiled=True)
    arrived = arrived.reshape(owners, shards, head_share * per_owner + stat_rows, HEAD_DIM)
    part_in = arrived[:, :, : head_share * per_owner].reshape(owners, shards, head_share, per_owner, HEAD_DIM)
    stat_in = arrived[:, :, head_share * per_owner :].reshape(owners * shards, stat_rows * HEAD_DIM)
    stats_in = join_three(
        stat_in[:, :stat_count].reshape(owners * shards, 3, 2, head_share, per_owner)
    ).reshape(owners, shards, 2, head_share, per_owner)
    maxima = stats_in[:, :, 0]
    totals = stats_in[:, :, 1]
    row_best = jnp.max(maxima, axis=1)
    weight = jnp.exp(maxima - row_best[:, None])
    total_sum = jnp.sum(totals * weight, axis=1)
    numerator = jnp.sum(part_in.astype(jnp.float32) * weight[..., None], axis=1)
    attended = numerator / total_sum[..., None]
    attended_low = jnp.transpose(attended, (0, 2, 1, 3)).reshape(row_count, share_width)
    return attended_low.astype(jnp.bfloat16)


def solution(mesh):
    return jax.shard_map(
        local,
        mesh=mesh,
        in_specs=(P("row", None), P("ctx", None), P("ctx", None), P("row", None), P("row")),
        out_specs=P("row", "ctx"),
        check_vma=False,
    )
```

```python
import functools

import jax
import jax.numpy as jnp
from jax import lax
from jax.experimental import pallas as pl
from jax.experimental.pallas import tpu as pltpu
from jax.sharding import PartitionSpec as P

HEADS = 16
HEAD_DIM = 128
BLOCK = 128


masked_fill = -1e30


def attention_kernel(shape, list_ref, count_ref, first_ref, q_ref, k_ref, v_ref, part_ref, stat_ref,
                     bias_ref, dead_ref, out_scr, stat_scr):
    rows, owners, per_owner, head_share, q_blocks, k_blocks, max_sel = shape

    @pl.when(pl.program_id(0) == 0)
    def _():
        first = first_ref[0]
        for a in range(q_blocks):
            any_live = jnp.int32(0)
            for b in range(k_blocks):
                hit = jnp.int32(0)
                for slot in range(max_sel):
                    found = (list_ref[a, slot] == first + b) & (slot < count_ref[a])
                    hit = jnp.maximum(hit, jnp.where(found, 1, 0).astype(jnp.int32))
                any_live = jnp.maximum(any_live, hit)
                bias_ref[a * k_blocks + b] = jnp.where(hit > 0, 0.0, masked_fill).astype(jnp.float32)
            dead_ref[a] = jnp.where(any_live > 0, 0.0, jnp.inf).astype(jnp.float32)
        stat_scr[...] = jnp.zeros_like(stat_scr)

    score_scale = 1.0 / HEAD_DIM**0.5
    for hl in range(head_share):
        cols = slice(hl * HEAD_DIM, (hl + 1) * HEAD_DIM)
        for a in range(q_blocks):
            here = slice(a * BLOCK, (a + 1) * BLOCK)
            scores = lax.dot_general(
                q_ref[here, cols], k_ref[:, cols], (((1,), (1,)), ((), ())), preferred_element_type=jnp.float32
            )
            bias = jnp.concatenate(
                [jnp.full((1, BLOCK), bias_ref[a * k_blocks + b], jnp.float32) for b in range(k_blocks)], axis=1
            )
            scores = scores * score_scale + bias
            seg_max = jnp.max(scores, axis=1, keepdims=True)
            probs = jnp.exp(scores - (seg_max + dead_ref[a]))
            seg_total = jnp.sum(probs, axis=1, keepdims=True)
            out_scr[here, :] = jnp.dot(
                probs.astype(jnp.bfloat16), v_ref[:, cols], preferred_element_type=jnp.float32
            )
            stat_scr[here, hl : hl + 1] = seg_max
            stat_scr[here, head_share + hl : head_share + hl + 1] = seg_total
        for r in range(owners):
            part_ref[r, hl * per_owner : (hl + 1) * per_owner, :] = out_scr[
                pl.ds(r, per_owner, stride=owners), :
            ].astype(jnp.bfloat16)
    stat_ref[0] = jnp.transpose(stat_scr[...])[: 2 * head_share]


def local_attention(queries, keys, values, block_list, block_count, first_block, owners, shards, dest_rows):
    rows = queries.shape[0]
    ctx_span = keys.shape[0]
    per_owner = rows // owners
    head_share = HEADS // shards
    share_width = head_share * HEAD_DIM
    q_blocks = rows // BLOCK
    k_blocks = ctx_span // BLOCK
    max_sel = block_list.shape[1]
    shape = (rows, owners, per_owner, head_share, q_blocks, k_blocks, max_sel)
    grid_spec = pltpu.PrefetchScalarGridSpec(
        num_scalar_prefetch=3,
        grid=(shards,),
        in_specs=[
            pl.BlockSpec((rows, share_width), lambda g, *_: (0, g)),
            pl.BlockSpec((ctx_span, share_width), lambda g, *_: (0, g)),
            pl.BlockSpec((ctx_span, share_width), lambda g, *_: (0, g)),
        ],
        out_specs=[
            pl.BlockSpec((owners, None, head_share * per_owner, HEAD_DIM), lambda g, *_: (0, g, 0, 0)),
            pl.BlockSpec((1, 2 * head_share, rows), lambda g, *_: (g, 0, 0)),
        ],
        scratch_shapes=[
            pltpu.SMEM((q_blocks * k_blocks,), jnp.float32),
            pltpu.SMEM((q_blocks,), jnp.float32),
            pltpu.VMEM((rows, HEAD_DIM), jnp.float32),
            pltpu.VMEM((rows, HEAD_DIM), jnp.float32),
        ],
    )
    flops = 4 * HEADS * rows * ctx_span * HEAD_DIM
    return pl.pallas_call(
        functools.partial(attention_kernel, shape),
        grid_spec=grid_spec,
        out_shape=[
            jax.ShapeDtypeStruct((owners, shards, dest_rows, HEAD_DIM), jnp.bfloat16),
            jax.ShapeDtypeStruct((shards, 2 * head_share, rows), jnp.float32),
        ],
        compiler_params=pltpu.CompilerParams(dimension_semantics=("arbitrary",)),
        cost_estimate=pl.CostEstimate(
            flops=flops,
            transcendentals=HEADS * rows * ctx_span,
            bytes_accessed=2 * (queries.size + keys.size + values.size) + 2 * rows * HEADS * HEAD_DIM,
        ),
    )(block_list, block_count, first_block, queries, keys, values)


def split_three(x):
    hi = lax.reduce_precision(x, exponent_bits=8, mantissa_bits=7)
    rest = x - hi
    mid = lax.reduce_precision(rest, exponent_bits=8, mantissa_bits=7)
    lo = lax.reduce_precision(rest - mid, exponent_bits=8, mantissa_bits=7)
    return jnp.stack([hi, mid, lo], axis=1).astype(jnp.bfloat16)


def join_three(parts):
    parts = parts.astype(jnp.float32)
    return (parts[:, 0] + parts[:, 1]) + parts[:, 2]


def local(queries, keys, values, block_list, block_count):
    row_count = queries.shape[0]
    ctx_span = keys.shape[0]
    shards = lax.axis_size("ctx")
    owners = lax.axis_size("row")
    per_owner = row_count // owners
    head_share = HEADS // shards
    share_width = head_share * HEAD_DIM
    blocks_here = ctx_span // BLOCK
    first_block = (lax.axis_index("ctx") * blocks_here).astype(jnp.int32).reshape(1)
    stat_count = 3 * 2 * head_share * per_owner
    stat_rows = -(-stat_count // HEAD_DIM)
    part_rows = head_share * per_owner
    part, stat = local_attention(
        queries, keys, values, block_list.astype(jnp.int32), block_count.astype(jnp.int32), first_block,
        owners, shards, part_rows + stat_rows,
    )
    stats = jnp.transpose(stat.reshape(shards, 2, head_share, per_owner, owners), (4, 0, 1, 2, 3))
    stats = stats.reshape(owners * shards, 2, head_share, per_owner)
    stat_low = split_three(stats).reshape(owners * shards, stat_count)
    stat_low = jnp.pad(stat_low, ((0, 0), (0, stat_rows * HEAD_DIM - stat_count)))
    payload = lax.dynamic_update_slice_in_dim(
        part.reshape(owners * shards, part_rows + stat_rows, HEAD_DIM),
        stat_low.reshape(owners * shards, stat_rows, HEAD_DIM),
        part_rows,
        axis=1,
    )
    arrived = lax.all_to_all(payload, ("row", "ctx"), 0, 0, tiled=True)
    arrived = arrived.reshape(owners, shards, head_share * per_owner + stat_rows, HEAD_DIM)
    part_in = arrived[:, :, : head_share * per_owner].reshape(owners, shards, head_share, per_owner, HEAD_DIM)
    stat_in = arrived[:, :, head_share * per_owner :].reshape(owners * shards, stat_rows * HEAD_DIM)
    stats_in = join_three(
        stat_in[:, :stat_count].reshape(owners * shards, 3, 2, head_share, per_owner)
    ).reshape(owners, shards, 2, head_share, per_owner)
    maxima = stats_in[:, :, 0]
    totals = stats_in[:, :, 1]
    row_best = jnp.max(maxima, axis=1)
    weight = jnp.exp(maxima - row_best[:, None])
    total_sum = jnp.sum(totals * weight, axis=1)
    numerator = jnp.sum(part_in.astype(jnp.float32) * weight[..., None], axis=1)
    attended = numerator / total_sum[..., None]
    attended_low = jnp.transpose(attended, (0, 2, 1, 3)).reshape(row_count, share_width)
    return attended_low.astype(jnp.bfloat16)


def solution(mesh):
    return jax.shard_map(
        local,
        mesh=mesh,
        in_specs=(P("row", None), P("ctx", None), P("ctx", None), P("row", None), P("row")),
        out_specs=P("row", "ctx"),
        check_vma=False,
    )
```

```python
import functools

import jax
import jax.numpy as jnp
from jax import lax
from jax.experimental import pallas as pl
from jax.experimental.pallas import tpu as pltpu
from jax.sharding import PartitionSpec as P

HEADS = 16
HEAD_DIM = 128
BLOCK = 128


masked_fill = -1e30


def attention_kernel(shape, list_ref, count_ref, first_ref, q_ref, k_ref, v_ref, part_ref, stat_ref,
                     bias_ref, any_ref):
    rows, head_share, q_blocks, k_blocks, max_sel = shape

    @pl.when(pl.program_id(0) == 0)
    def _():
        first = first_ref[0]
        for a in range(q_blocks):
            any_live = jnp.int32(0)
            for b in range(k_blocks):
                hit = jnp.int32(0)
                for slot in range(max_sel):
                    found = (list_ref[a, slot] == first + b) & (slot < count_ref[a])
                    hit = jnp.maximum(hit, jnp.where(found, 1, 0).astype(jnp.int32))
                any_live = jnp.maximum(any_live, hit)
                bias = jnp.where(hit > 0, 0.0, masked_fill).astype(jnp.float32)
                bias_ref[a * BLOCK : (a + 1) * BLOCK, b * BLOCK : (b + 1) * BLOCK] = jnp.full(
                    (BLOCK, BLOCK), bias, jnp.float32
                )
            dead = jnp.where(any_live > 0, 0.0, jnp.inf).astype(jnp.float32)
            any_ref[a * BLOCK : (a + 1) * BLOCK, :] = jnp.full((BLOCK, HEAD_DIM), dead, jnp.float32)

    score_scale = 1.0 / HEAD_DIM**0.5
    dead_row = any_ref[:, 0:1]
    lane = lax.broadcasted_iota(jnp.int32, (rows, HEAD_DIM), 1)
    stats = jnp.zeros((rows, HEAD_DIM), jnp.float32)
    for hl in range(head_share):
        cols = slice(hl * HEAD_DIM, (hl + 1) * HEAD_DIM)
        scores = lax.dot_general(
            q_ref[:, cols], k_ref[:, cols], (((1,), (1,)), ((), ())), preferred_element_type=jnp.float32
        )
        scores = scores * score_scale + bias_ref[...]
        seg_max = jnp.max(scores, axis=1, keepdims=True)
        probs = jnp.exp(scores - (seg_max + dead_row))
        seg_total = jnp.sum(probs, axis=1, keepdims=True)
        seg_out = jnp.dot(probs.astype(jnp.bfloat16), v_ref[:, cols], preferred_element_type=jnp.float32)
        part_ref[hl] = seg_out.astype(jnp.bfloat16)
        stats = jnp.where(lane == hl, seg_max, stats)
        stats = jnp.where(lane == head_share + hl, seg_total, stats)
    stat_ref[0] = jnp.transpose(stats)[: 2 * head_share]


def local_attention(queries, keys, values, block_list, block_count, first_block, shards):
    rows = queries.shape[0]
    ctx_span = keys.shape[0]
    head_share = HEADS // shards
    share_width = head_share * HEAD_DIM
    q_blocks = rows // BLOCK
    k_blocks = ctx_span // BLOCK
    max_sel = block_list.shape[1]
    shape = (rows, head_share, q_blocks, k_blocks, max_sel)
    grid_spec = pltpu.PrefetchScalarGridSpec(
        num_scalar_prefetch=3,
        grid=(shards,),
        in_specs=[
            pl.BlockSpec((rows, share_width), lambda g, *_: (0, g)),
            pl.BlockSpec((ctx_span, share_width), lambda g, *_: (0, g)),
            pl.BlockSpec((ctx_span, share_width), lambda g, *_: (0, g)),
        ],
        out_specs=[
            pl.BlockSpec((head_share, rows, HEAD_DIM), lambda g, *_: (g, 0, 0)),
            pl.BlockSpec((1, 2 * head_share, rows), lambda g, *_: (g, 0, 0)),
        ],
        scratch_shapes=[
            pltpu.VMEM((rows, ctx_span), jnp.float32),
            pltpu.VMEM((rows, HEAD_DIM), jnp.float32),
        ],
    )
    flops = 4 * HEADS * rows * ctx_span * HEAD_DIM
    return pl.pallas_call(
        functools.partial(attention_kernel, shape),
        grid_spec=grid_spec,
        out_shape=[
            jax.ShapeDtypeStruct((HEADS, rows, HEAD_DIM), jnp.bfloat16),
            jax.ShapeDtypeStruct((shards, 2 * head_share, rows), jnp.float32),
        ],
        compiler_params=pltpu.CompilerParams(dimension_semantics=("arbitrary",)),
        cost_estimate=pl.CostEstimate(
            flops=flops,
            transcendentals=HEADS * rows * ctx_span,
            bytes_accessed=2 * (queries.size + keys.size + values.size) + 2 * rows * HEADS * HEAD_DIM,
        ),
    )(block_list, block_count, first_block, queries, keys, values)


def split_three(x):
    hi = lax.reduce_precision(x, exponent_bits=8, mantissa_bits=7)
    rest = x - hi
    mid = lax.reduce_precision(rest, exponent_bits=8, mantissa_bits=7)
    lo = lax.reduce_precision(rest - mid, exponent_bits=8, mantissa_bits=7)
    return jnp.stack([hi, mid, lo], axis=1).astype(jnp.bfloat16)


def join_three(parts):
    parts = parts.astype(jnp.float32)
    return (parts[:, 0] + parts[:, 1]) + parts[:, 2]


def local(queries, keys, values, block_list, block_count):
    row_count = queries.shape[0]
    ctx_span = keys.shape[0]
    shards = lax.axis_size("ctx")
    owners = lax.axis_size("row")
    per_owner = row_count // owners
    head_share = HEADS // shards
    share_width = head_share * HEAD_DIM
    blocks_here = ctx_span // BLOCK
    first_block = (lax.axis_index("ctx") * blocks_here).astype(jnp.int32).reshape(1)
    part, stat = local_attention(
        queries, keys, values, block_list.astype(jnp.int32), block_count.astype(jnp.int32), first_block, shards
    )
    part_low = part.reshape(shards, head_share, per_owner, owners, HEAD_DIM)
    part_low = jnp.transpose(part_low, (3, 0, 2, 1, 4)).reshape(
        owners * shards, head_share * per_owner, HEAD_DIM
    )
    stats = jnp.transpose(stat.reshape(shards, 2, head_share, per_owner, owners), (4, 0, 1, 2, 3))
    stats = stats.reshape(owners * shards, 2, head_share, per_owner)
    stat_count = 3 * 2 * head_share * per_owner
    stat_rows = -(-stat_count // HEAD_DIM)
    stat_low = split_three(stats).reshape(owners * shards, stat_count)
    stat_low = jnp.pad(stat_low, ((0, 0), (0, stat_rows * HEAD_DIM - stat_count)))
    payload = jnp.concatenate(
        [part_low, stat_low.reshape(owners * shards, stat_rows, HEAD_DIM)], axis=1
    )
    arrived = lax.all_to_all(payload, ("row", "ctx"), 0, 0, tiled=True)
    arrived = arrived.reshape(owners, shards, head_share * per_owner + stat_rows, HEAD_DIM)
    part_in = arrived[:, :, : head_share * per_owner].reshape(owners, shards, per_owner, head_share, HEAD_DIM)
    stat_in = arrived[:, :, head_share * per_owner :].reshape(owners * shards, stat_rows * HEAD_DIM)
    stats_in = join_three(
        stat_in[:, :stat_count].reshape(owners * shards, 3, 2, head_share, per_owner)
    ).reshape(owners, shards, 2, head_share, per_owner)
    maxima = stats_in[:, :, 0]
    totals = stats_in[:, :, 1]
    row_best = jnp.max(maxima, axis=1)
    weight = jnp.exp(maxima - row_best[:, None])
    total_sum = jnp.sum(totals * weight, axis=1)
    weight = jnp.swapaxes(weight, 2, 3)
    total_sum = jnp.swapaxes(total_sum, 1, 2)
    numerator = jnp.sum(part_in.astype(jnp.float32) * weight[..., None], axis=1)
    attended = numerator / total_sum[..., None]
    attended_low = attended.reshape(row_count, share_width)
    return attended_low.astype(jnp.bfloat16)


def solution(mesh):
    return jax.shard_map(
        local,
        mesh=mesh,
        in_specs=(P("row", None), P("ctx", None), P("ctx", None), P("row", None), P("row")),
        out_specs=P("row", "ctx"),
        check_vma=False,
    )
```

```python
import functools

import jax
import jax.numpy as jnp
from jax import lax
from jax.experimental import pallas as pl
from jax.experimental.pallas import tpu as pltpu
from jax.sharding import PartitionSpec as P

HEADS = 16
HEAD_DIM = 128
BLOCK = 128


masked_fill = -1e30


def attention_kernel(shape, list_ref, count_ref, first_ref, q_ref, k_ref, v_ref, part_ref, stat_ref,
                     bias_ref, dead_ref):
    rows, head_share, q_blocks, k_blocks, max_sel = shape

    @pl.when(pl.program_id(0) == 0)
    def _():
        first = first_ref[0]
        for a in range(q_blocks):
            any_live = jnp.int32(0)
            for b in range(k_blocks):
                hit = jnp.int32(0)
                for slot in range(max_sel):
                    found = (list_ref[a, slot] == first + b) & (slot < count_ref[a])
                    hit = jnp.maximum(hit, jnp.where(found, 1, 0).astype(jnp.int32))
                any_live = jnp.maximum(any_live, hit)
                bias = jnp.where(hit > 0, 0.0, masked_fill).astype(jnp.float32)
                bias_ref[b * BLOCK : (b + 1) * BLOCK, a * BLOCK : (a + 1) * BLOCK] = jnp.full(
                    (BLOCK, BLOCK), bias, jnp.float32
                )
            dead = jnp.where(any_live > 0, 0.0, jnp.inf).astype(jnp.float32)
            dead_ref[:, a * BLOCK : (a + 1) * BLOCK] = jnp.full((8, BLOCK), dead, jnp.float32)

    score_scale = 1.0 / HEAD_DIM**0.5
    dead_row = dead_ref[0:1, :]
    for hl in range(head_share):
        cols = slice(hl * HEAD_DIM, (hl + 1) * HEAD_DIM)
        scores = lax.dot_general(
            k_ref[:, cols], q_ref[:, cols], (((1,), (1,)), ((), ())), preferred_element_type=jnp.float32
        )
        scores = scores * score_scale + bias_ref[...]
        seg_max = jnp.max(scores, axis=0, keepdims=True)
        probs = jnp.exp(scores - (seg_max + dead_row))
        seg_total = jnp.sum(probs, axis=0, keepdims=True)
        seg_out = lax.dot_general(
            probs.astype(jnp.bfloat16), v_ref[:, cols], (((0,), (0,)), ((), ())),
            preferred_element_type=jnp.float32,
        )
        part_ref[hl] = seg_out.astype(jnp.bfloat16)
        stat_ref[0, hl : hl + 1, :] = seg_max
        stat_ref[0, head_share + hl : head_share + hl + 1, :] = seg_total


def local_attention(queries, keys, values, block_list, block_count, first_block, shards):
    rows = queries.shape[0]
    ctx_span = keys.shape[0]
    head_share = HEADS // shards
    share_width = head_share * HEAD_DIM
    q_blocks = rows // BLOCK
    k_blocks = ctx_span // BLOCK
    max_sel = block_list.shape[1]
    shape = (rows, head_share, q_blocks, k_blocks, max_sel)
    grid_spec = pltpu.PrefetchScalarGridSpec(
        num_scalar_prefetch=3,
        grid=(shards,),
        in_specs=[
            pl.BlockSpec((rows, share_width), lambda g, *_: (0, g)),
            pl.BlockSpec((ctx_span, share_width), lambda g, *_: (0, g)),
            pl.BlockSpec((ctx_span, share_width), lambda g, *_: (0, g)),
        ],
        out_specs=[
            pl.BlockSpec((head_share, rows, HEAD_DIM), lambda g, *_: (g, 0, 0)),
            pl.BlockSpec((1, 2 * head_share, rows), lambda g, *_: (g, 0, 0)),
        ],
        scratch_shapes=[
            pltpu.VMEM((ctx_span, rows), jnp.float32),
            pltpu.VMEM((8, rows), jnp.float32),
        ],
    )
    flops = 4 * HEADS * rows * ctx_span * HEAD_DIM
    return pl.pallas_call(
        functools.partial(attention_kernel, shape),
        grid_spec=grid_spec,
        out_shape=[
            jax.ShapeDtypeStruct((HEADS, rows, HEAD_DIM), jnp.bfloat16),
            jax.ShapeDtypeStruct((shards, 2 * head_share, rows), jnp.float32),
        ],
        compiler_params=pltpu.CompilerParams(dimension_semantics=("arbitrary",)),
        cost_estimate=pl.CostEstimate(
            flops=flops,
            transcendentals=HEADS * rows * ctx_span,
            bytes_accessed=2 * (queries.size + keys.size + values.size) + 2 * rows * HEADS * HEAD_DIM,
        ),
    )(block_list, block_count, first_block, queries, keys, values)


def split_three(x):
    hi = lax.reduce_precision(x, exponent_bits=8, mantissa_bits=7)
    rest = x - hi
    mid = lax.reduce_precision(rest, exponent_bits=8, mantissa_bits=7)
    lo = lax.reduce_precision(rest - mid, exponent_bits=8, mantissa_bits=7)
    return jnp.stack([hi, mid, lo], axis=1).astype(jnp.bfloat16)


def join_three(parts):
    parts = parts.astype(jnp.float32)
    return (parts[:, 0] + parts[:, 1]) + parts[:, 2]


def local(queries, keys, values, block_list, block_count):
    row_count = queries.shape[0]
    ctx_span = keys.shape[0]
    shards = lax.axis_size("ctx")
    owners = lax.axis_size("row")
    per_owner = row_count // owners
    head_share = HEADS // shards
    share_width = head_share * HEAD_DIM
    blocks_here = ctx_span // BLOCK
    first_block = (lax.axis_index("ctx") * blocks_here).astype(jnp.int32).reshape(1)
    part, stat = local_attention(
        queries, keys, values, block_list.astype(jnp.int32), block_count.astype(jnp.int32), first_block, shards
    )
    part_low = part.reshape(shards, head_share, per_owner, owners, HEAD_DIM)
    part_low = jnp.transpose(part_low, (3, 0, 1, 2, 4)).reshape(
        owners * shards, head_share * per_owner, HEAD_DIM
    )
    stats = jnp.transpose(stat.reshape(shards, 2, head_share, per_owner, owners), (4, 0, 1, 2, 3))
    stats = stats.reshape(owners * shards, 2, head_share, per_owner)
    stat_count = 3 * 2 * head_share * per_owner
    stat_rows = -(-stat_count // HEAD_DIM)
    stat_low = split_three(stats).reshape(owners * shards, stat_count)
    stat_low = jnp.pad(stat_low, ((0, 0), (0, stat_rows * HEAD_DIM - stat_count)))
    payload = jnp.concatenate(
        [part_low, stat_low.reshape(owners * shards, stat_rows, HEAD_DIM)], axis=1
    )
    arrived = lax.all_to_all(payload, ("row", "ctx"), 0, 0, tiled=True)
    arrived = arrived.reshape(owners, shards, head_share * per_owner + stat_rows, HEAD_DIM)
    part_in = arrived[:, :, : head_share * per_owner].reshape(owners, shards, head_share, per_owner, HEAD_DIM)
    stat_in = arrived[:, :, head_share * per_owner :].reshape(owners * shards, stat_rows * HEAD_DIM)
    stats_in = join_three(
        stat_in[:, :stat_count].reshape(owners * shards, 3, 2, head_share, per_owner)
    ).reshape(owners, shards, 2, head_share, per_owner)
    maxima = stats_in[:, :, 0]
    totals = stats_in[:, :, 1]
    row_best = jnp.max(maxima, axis=1)
    weight = jnp.exp(maxima - row_best[:, None])
    total_sum = jnp.sum(totals * weight, axis=1)
    numerator = jnp.sum(part_in.astype(jnp.float32) * weight[..., None], axis=1)
    attended = numerator / total_sum[..., None]
    attended_low = jnp.transpose(attended, (0, 2, 1, 3)).reshape(row_count, share_width)
    return attended_low.astype(jnp.bfloat16)


def solution(mesh):
    return jax.shard_map(
        local,
        mesh=mesh,
        in_specs=(P("row", None), P("ctx", None), P("ctx", None), P("row", None), P("row")),
        out_specs=P("row", "ctx"),
        check_vma=False,
    )
```

```python
import functools

import jax
import jax.numpy as jnp
from jax import lax
from jax.experimental import pallas as pl
from jax.experimental.pallas import tpu as pltpu
from jax.sharding import PartitionSpec as P

HEADS = 16
HEAD_DIM = 128
BLOCK = 128


masked_fill = -1e30


def attention_kernel(shape, list_ref, count_ref, first_ref, q_ref, k_ref, v_ref, part_ref, stat_ref,
                     bias_ref, dead_ref, perm_ref):
    rows, owners, per_owner, head_share, q_blocks, k_blocks, max_sel = shape

    @pl.when(pl.program_id(0) == 0)
    def _():
        first = first_ref[0]
        for a in range(q_blocks):
            any_live = jnp.int32(0)
            for b in range(k_blocks):
                hit = jnp.int32(0)
                for slot in range(max_sel):
                    found = (list_ref[a, slot] == first + b) & (slot < count_ref[a])
                    hit = jnp.maximum(hit, jnp.where(found, 1, 0).astype(jnp.int32))
                any_live = jnp.maximum(any_live, hit)
                bias = jnp.where(hit > 0, 0.0, masked_fill).astype(jnp.float32)
                bias_ref[b * BLOCK : (b + 1) * BLOCK, a * BLOCK : (a + 1) * BLOCK] = jnp.full(
                    (BLOCK, BLOCK), bias, jnp.float32
                )
            dead = jnp.where(any_live > 0, 0.0, jnp.inf).astype(jnp.float32)
            dead_ref[:, a * BLOCK : (a + 1) * BLOCK] = jnp.full((8, BLOCK), dead, jnp.float32)
        pos = lax.broadcasted_iota(jnp.int32, (rows, rows), 0)
        frame = lax.broadcasted_iota(jnp.int32, (rows, rows), 1)
        perm_ref[...] = jnp.where(
            frame == (pos % per_owner) * owners + pos // per_owner, 1.0, 0.0
        ).astype(jnp.bfloat16)

    score_scale = 1.0 / HEAD_DIM**0.5
    dead_row = dead_ref[0:1, :]
    for hl in range(head_share):
        cols = slice(hl * HEAD_DIM, (hl + 1) * HEAD_DIM)
        scores = lax.dot_general(
            k_ref[:, cols], q_ref[:, cols], (((1,), (1,)), ((), ())), preferred_element_type=jnp.float32
        )
        scores = scores * score_scale + bias_ref[...]
        seg_max = jnp.max(scores, axis=0, keepdims=True)
        probs = jnp.exp(scores - (seg_max + dead_row))
        seg_total = jnp.sum(probs, axis=0, keepdims=True)
        seg_out = lax.dot_general(
            probs.astype(jnp.bfloat16), v_ref[:, cols], (((0,), (0,)), ((), ())),
            preferred_element_type=jnp.float32,
        )
        seg_out = jnp.dot(perm_ref[...], seg_out.astype(jnp.bfloat16), preferred_element_type=jnp.float32)
        part_ref[:, hl] = seg_out.reshape(owners, per_owner, HEAD_DIM).astype(jnp.bfloat16)
        stat_ref[0, hl : hl + 1, :] = seg_max
        stat_ref[0, head_share + hl : head_share + hl + 1, :] = seg_total


def local_attention(queries, keys, values, block_list, block_count, first_block, owners, shards):
    rows = queries.shape[0]
    per_owner = rows // owners
    ctx_span = keys.shape[0]
    head_share = HEADS // shards
    share_width = head_share * HEAD_DIM
    q_blocks = rows // BLOCK
    k_blocks = ctx_span // BLOCK
    max_sel = block_list.shape[1]
    shape = (rows, owners, per_owner, head_share, q_blocks, k_blocks, max_sel)
    grid_spec = pltpu.PrefetchScalarGridSpec(
        num_scalar_prefetch=3,
        grid=(shards,),
        in_specs=[
            pl.BlockSpec((rows, share_width), lambda g, *_: (0, g)),
            pl.BlockSpec((ctx_span, share_width), lambda g, *_: (0, g)),
            pl.BlockSpec((ctx_span, share_width), lambda g, *_: (0, g)),
        ],
        out_specs=[
            pl.BlockSpec((owners, head_share, per_owner, HEAD_DIM), lambda g, *_: (0, g, 0, 0)),
            pl.BlockSpec((1, 2 * head_share, rows), lambda g, *_: (g, 0, 0)),
        ],
        scratch_shapes=[
            pltpu.VMEM((ctx_span, rows), jnp.float32),
            pltpu.VMEM((8, rows), jnp.float32),
            pltpu.VMEM((rows, rows), jnp.bfloat16),
        ],
    )
    flops = 4 * HEADS * rows * ctx_span * HEAD_DIM
    return pl.pallas_call(
        functools.partial(attention_kernel, shape),
        grid_spec=grid_spec,
        out_shape=[
            jax.ShapeDtypeStruct((owners, HEADS, per_owner, HEAD_DIM), jnp.bfloat16),
            jax.ShapeDtypeStruct((shards, 2 * head_share, rows), jnp.float32),
        ],
        compiler_params=pltpu.CompilerParams(dimension_semantics=("arbitrary",)),
        cost_estimate=pl.CostEstimate(
            flops=flops,
            transcendentals=HEADS * rows * ctx_span,
            bytes_accessed=2 * (queries.size + keys.size + values.size) + 2 * rows * HEADS * HEAD_DIM,
        ),
    )(block_list, block_count, first_block, queries, keys, values)


def split_three(x):
    hi = lax.reduce_precision(x, exponent_bits=8, mantissa_bits=7)
    rest = x - hi
    mid = lax.reduce_precision(rest, exponent_bits=8, mantissa_bits=7)
    lo = lax.reduce_precision(rest - mid, exponent_bits=8, mantissa_bits=7)
    return jnp.stack([hi, mid, lo], axis=1).astype(jnp.bfloat16)


def join_three(parts):
    parts = parts.astype(jnp.float32)
    return (parts[:, 0] + parts[:, 1]) + parts[:, 2]


def local(queries, keys, values, block_list, block_count):
    row_count = queries.shape[0]
    ctx_span = keys.shape[0]
    shards = lax.axis_size("ctx")
    owners = lax.axis_size("row")
    per_owner = row_count // owners
    head_share = HEADS // shards
    share_width = head_share * HEAD_DIM
    blocks_here = ctx_span // BLOCK
    first_block = (lax.axis_index("ctx") * blocks_here).astype(jnp.int32).reshape(1)
    part, stat = local_attention(
        queries, keys, values, block_list.astype(jnp.int32), block_count.astype(jnp.int32), first_block, owners, shards
    )
    part_low = part.reshape(owners * shards, head_share * per_owner, HEAD_DIM)
    stats = jnp.transpose(stat.reshape(shards, 2, head_share, per_owner, owners), (4, 0, 1, 2, 3))
    stats = stats.reshape(owners * shards, 2, head_share, per_owner)
    stat_count = 3 * 2 * head_share * per_owner
    stat_rows = -(-stat_count // HEAD_DIM)
    stat_low = split_three(stats).reshape(owners * shards, stat_count)
    stat_low = jnp.pad(stat_low, ((0, 0), (0, stat_rows * HEAD_DIM - stat_count)))
    payload = jnp.concatenate(
        [part_low, stat_low.reshape(owners * shards, stat_rows, HEAD_DIM)], axis=1
    )
    arrived = lax.all_to_all(payload, ("row", "ctx"), 0, 0, tiled=True)
    arrived = arrived.reshape(owners, shards, head_share * per_owner + stat_rows, HEAD_DIM)
    part_in = arrived[:, :, : head_share * per_owner].reshape(owners, shards, head_share, per_owner, HEAD_DIM)
    stat_in = arrived[:, :, head_share * per_owner :].reshape(owners * shards, stat_rows * HEAD_DIM)
    stats_in = join_three(
        stat_in[:, :stat_count].reshape(owners * shards, 3, 2, head_share, per_owner)
    ).reshape(owners, shards, 2, head_share, per_owner)
    maxima = stats_in[:, :, 0]
    totals = stats_in[:, :, 1]
    row_best = jnp.max(maxima, axis=1)
    weight = jnp.exp(maxima - row_best[:, None])
    total_sum = jnp.sum(totals * weight, axis=1)
    numerator = jnp.sum(part_in.astype(jnp.float32) * weight[..., None], axis=1)
    attended = numerator / total_sum[..., None]
    attended_low = jnp.transpose(attended, (0, 2, 1, 3)).reshape(row_count, share_width)
    return attended_low.astype(jnp.bfloat16)


def solution(mesh):
    return jax.shard_map(
        local,
        mesh=mesh,
        in_specs=(P("row", None), P("ctx", None), P("ctx", None), P("row", None), P("row")),
        out_specs=P("row", "ctx"),
        check_vma=False,
    )
```

```python
import functools

import jax
import jax.numpy as jnp
from jax import lax
from jax.experimental import pallas as pl
from jax.experimental.pallas import tpu as pltpu
from jax.sharding import PartitionSpec as P

HEADS = 16
HEAD_DIM = 128
BLOCK = 128


masked_fill = -1e30


def attention_kernel(shape, list_ref, count_ref, first_ref, q_ref, k_ref, v_ref, part_ref, stat_ref,
                     bias_ref, dead_ref):
    rows, head_share, q_blocks, k_blocks, max_sel = shape

    @pl.when(pl.program_id(0) == 0)
    def _():
        first = first_ref[0]
        for a in range(q_blocks):
            any_live = jnp.int32(0)
            for b in range(k_blocks):
                hit = jnp.int32(0)
                for slot in range(max_sel):
                    found = (list_ref[a, slot] == first + b) & (slot < count_ref[a])
                    hit = jnp.maximum(hit, jnp.where(found, 1, 0).astype(jnp.int32))
                any_live = jnp.maximum(any_live, hit)
                bias = jnp.where(hit > 0, 0.0, masked_fill).astype(jnp.float32)
                bias_ref[b * BLOCK : (b + 1) * BLOCK, a * BLOCK : (a + 1) * BLOCK] = jnp.full(
                    (BLOCK, BLOCK), bias, jnp.float32
                )
            dead = jnp.where(any_live > 0, 0.0, jnp.inf).astype(jnp.float32)
            dead_ref[:, a * BLOCK : (a + 1) * BLOCK] = jnp.full((8, BLOCK), dead, jnp.float32)

    score_scale = 1.0 / HEAD_DIM**0.5
    dead_row = dead_ref[0:1, :]
    for hl in range(head_share):
        cols = slice(hl * HEAD_DIM, (hl + 1) * HEAD_DIM)
        scores = lax.dot_general(
            k_ref[:, cols], q_ref[:, cols], (((1,), (1,)), ((), ())), preferred_element_type=jnp.float32
        )
        scores = scores * score_scale + bias_ref[...]
        seg_max = jnp.max(scores, axis=0, keepdims=True)
        probs = jnp.exp(scores - (seg_max + dead_row))
        seg_total = jnp.sum(probs, axis=0, keepdims=True)
        seg_out = lax.dot_general(
            probs.astype(jnp.bfloat16), v_ref[:, cols], (((0,), (0,)), ((), ())),
            preferred_element_type=jnp.float32,
        )
        part_ref[hl] = seg_out.astype(jnp.bfloat16)
        stat_ref[0, hl : hl + 1, :] = seg_max
        stat_ref[0, head_share + hl : head_share + hl + 1, :] = seg_total


def local_attention(queries, keys, values, block_list, block_count, first_block, shards):
    rows = queries.shape[0]
    ctx_span = keys.shape[0]
    head_share = HEADS // shards
    share_width = head_share * HEAD_DIM
    q_blocks = rows // BLOCK
    k_blocks = ctx_span // BLOCK
    max_sel = block_list.shape[1]
    shape = (rows, head_share, q_blocks, k_blocks, max_sel)
    grid_spec = pltpu.PrefetchScalarGridSpec(
        num_scalar_prefetch=3,
        grid=(shards,),
        in_specs=[
            pl.BlockSpec((rows, share_width), lambda g, *_: (0, g)),
            pl.BlockSpec((ctx_span, share_width), lambda g, *_: (0, g)),
            pl.BlockSpec((ctx_span, share_width), lambda g, *_: (0, g)),
        ],
        out_specs=[
            pl.BlockSpec((head_share, rows, HEAD_DIM), lambda g, *_: (g, 0, 0)),
            pl.BlockSpec((1, 2 * head_share, rows), lambda g, *_: (g, 0, 0)),
        ],
        scratch_shapes=[
            pltpu.VMEM((ctx_span, rows), jnp.float32),
            pltpu.VMEM((8, rows), jnp.float32),
        ],
    )
    flops = 4 * HEADS * rows * ctx_span * HEAD_DIM
    return pl.pallas_call(
        functools.partial(attention_kernel, shape),
        grid_spec=grid_spec,
        out_shape=[
            jax.ShapeDtypeStruct((HEADS, rows, HEAD_DIM), jnp.bfloat16),
            jax.ShapeDtypeStruct((shards, 2 * head_share, rows), jnp.float32),
        ],
        compiler_params=pltpu.CompilerParams(dimension_semantics=("arbitrary",)),
        cost_estimate=pl.CostEstimate(
            flops=flops,
            transcendentals=HEADS * rows * ctx_span,
            bytes_accessed=2 * (queries.size + keys.size + values.size) + 2 * rows * HEADS * HEAD_DIM,
        ),
    )(block_list, block_count, first_block, queries, keys, values)


def combine_kernel(shape, arr_ref, out_ref):
    owners, shards, per_owner, head_share, part_rows, stat_rows = shape
    share = head_share * per_owner

    def stat_column(stat_t, k):
        base = k * share
        if share % HEAD_DIM == 0:
            return stat_t[:, base // HEAD_DIM : base // HEAD_DIM + 1]
        return stat_t[base % HEAD_DIM : base % HEAD_DIM + share, base // HEAD_DIM : base // HEAD_DIM + 1]

    def body(r, carry):
        maxima, totals = [], []
        for c in range(shards):
            stat_t = jnp.transpose(arr_ref[r, c, part_rows:, :].astype(jnp.float32))
            parts = [[stat_column(stat_t, part * 2 + kind) for kind in range(2)] for part in range(3)]
            maxima.append((parts[0][0] + parts[1][0]) + parts[2][0])
            totals.append((parts[0][1] + parts[1][1]) + parts[2][1])
        best = maxima[0]
        for c in range(1, shards):
            best = jnp.maximum(best, maxima[c])
        total = None
        numer = None
        for c in range(shards):
            weight = jnp.exp(maxima[c] - best)
            term = totals[c] * weight
            total = term if total is None else total + term
            piece = arr_ref[r, c, :part_rows, :].astype(jnp.float32) * weight
            numer = piece if numer is None else numer + piece
        attended = (numer / total).astype(jnp.bfloat16)
        start = pl.multiple_of(r * per_owner, per_owner)
        for hl in range(head_share):
            out_ref[pl.ds(start, per_owner), hl * HEAD_DIM : (hl + 1) * HEAD_DIM] = attended[
                hl * per_owner : (hl + 1) * per_owner
            ]
        return carry

    lax.fori_loop(0, owners, body, 0)


def combine(arrived, owners, shards, per_owner, head_share, part_rows, stat_rows):
    shape = (owners, shards, per_owner, head_share, part_rows, stat_rows)
    assert (head_share * per_owner) % HEAD_DIM == 0 or HEAD_DIM % (head_share * per_owner) == 0
    return pl.pallas_call(
        functools.partial(combine_kernel, shape),
        in_specs=[pl.BlockSpec(memory_space=pltpu.VMEM)],
        out_specs=pl.BlockSpec(memory_space=pltpu.VMEM),
        out_shape=jax.ShapeDtypeStruct((owners * per_owner, head_share * HEAD_DIM), jnp.bfloat16),
        cost_estimate=pl.CostEstimate(
            flops=3 * arrived.size, transcendentals=owners * shards * 128, bytes_accessed=2 * arrived.size
        ),
    )(arrived.reshape(owners, shards, part_rows + stat_rows, HEAD_DIM))


def split_three(x):
    hi = lax.reduce_precision(x, exponent_bits=8, mantissa_bits=7)
    rest = x - hi
    mid = lax.reduce_precision(rest, exponent_bits=8, mantissa_bits=7)
    lo = lax.reduce_precision(rest - mid, exponent_bits=8, mantissa_bits=7)
    return jnp.stack([hi, mid, lo], axis=1).astype(jnp.bfloat16)


def join_three(parts):
    parts = parts.astype(jnp.float32)
    return (parts[:, 0] + parts[:, 1]) + parts[:, 2]


def local(queries, keys, values, block_list, block_count):
    row_count = queries.shape[0]
    ctx_span = keys.shape[0]
    shards = lax.axis_size("ctx")
    owners = lax.axis_size("row")
    per_owner = row_count // owners
    head_share = HEADS // shards
    share_width = head_share * HEAD_DIM
    blocks_here = ctx_span // BLOCK
    first_block = (lax.axis_index("ctx") * blocks_here).astype(jnp.int32).reshape(1)
    part, stat = local_attention(
        queries, keys, values, block_list.astype(jnp.int32), block_count.astype(jnp.int32), first_block, shards
    )
    part_low = part.reshape(shards, head_share, per_owner, owners, HEAD_DIM)
    part_low = jnp.transpose(part_low, (3, 0, 1, 2, 4)).reshape(
        owners * shards, head_share * per_owner, HEAD_DIM
    )
    stats = jnp.transpose(stat.reshape(shards, 2, head_share, per_owner, owners), (4, 0, 1, 2, 3))
    stats = stats.reshape(owners * shards, 2, head_share, per_owner)
    stat_count = 3 * 2 * head_share * per_owner
    stat_rows = -(-stat_count // HEAD_DIM)
    stat_low = split_three(stats).reshape(owners * shards, stat_count)
    stat_low = jnp.pad(stat_low, ((0, 0), (0, stat_rows * HEAD_DIM - stat_count)))
    payload = jnp.concatenate(
        [part_low, stat_low.reshape(owners * shards, stat_rows, HEAD_DIM)], axis=1
    )
    arrived = lax.all_to_all(payload, ("row", "ctx"), 0, 0, tiled=True)
    return combine(arrived, owners, shards, per_owner, head_share, head_share * per_owner, stat_rows)


def solution(mesh):
    return jax.shard_map(
        local,
        mesh=mesh,
        in_specs=(P("row", None), P("ctx", None), P("ctx", None), P("row", None), P("row")),
        out_specs=P("row", "ctx"),
        check_vma=False,
    )
```

```python
import functools

import jax
import jax.numpy as jnp
from jax import lax
from jax.experimental import pallas as pl
from jax.experimental.pallas import tpu as pltpu
from jax.sharding import PartitionSpec as P

HEADS = 16
HEAD_DIM = 128
BLOCK = 128


masked_fill = -1e30


def attention_kernel(shape, list_ref, count_ref, first_ref, q_ref, k_ref, v_ref, part_ref, stat_ref,
                     live_ref, score_scr, max_scr, total_scr, out_scr):
    rows, head_share, q_blocks, k_blocks, max_sel = shape

    @pl.when(pl.program_id(0) == 0)
    def _():
        first = first_ref[0]
        for a in range(q_blocks):
            for b in range(k_blocks):
                hit = jnp.int32(0)
                for slot in range(max_sel):
                    found = (list_ref[a, slot] == first + b) & (slot < count_ref[a])
                    hit = jnp.maximum(hit, jnp.where(found, 1, 0).astype(jnp.int32))
                live_ref[a * k_blocks + b] = hit

    score_scale = 1.0 / HEAD_DIM**0.5
    for hl in range(head_share):
        cols = slice(hl * HEAD_DIM, (hl + 1) * HEAD_DIM)
        for a in range(q_blocks):
            qs = slice(a * BLOCK, (a + 1) * BLOCK)
            max_scr[...] = jnp.full(max_scr.shape, masked_fill, jnp.float32)
            total_scr[...] = jnp.zeros(total_scr.shape, jnp.float32)
            out_scr[...] = jnp.zeros(out_scr.shape, jnp.float32)
            for b in range(k_blocks):
                ks = slice(b * BLOCK, (b + 1) * BLOCK)

                @pl.when(live_ref[a * k_blocks + b] > 0)
                def _():
                    tile = lax.dot_general(
                        k_ref[ks, cols], q_ref[qs, cols], (((1,), (1,)), ((), ())),
                        preferred_element_type=jnp.float32,
                    ) * score_scale
                    score_scr[ks, :] = tile
                    max_scr[...] = jnp.maximum(max_scr[...], jnp.max(tile, axis=0, keepdims=True))

            seg_max = max_scr[...]
            for b in range(k_blocks):
                ks = slice(b * BLOCK, (b + 1) * BLOCK)

                @pl.when(live_ref[a * k_blocks + b] > 0)
                def _():
                    probs = jnp.exp(score_scr[ks, :] - seg_max)
                    total_scr[...] += jnp.sum(probs, axis=0, keepdims=True)
                    out_scr[...] += lax.dot_general(
                        probs.astype(jnp.bfloat16), v_ref[ks, cols], (((0,), (0,)), ((), ())),
                        preferred_element_type=jnp.float32,
                    )

            part_ref[hl, qs, :] = out_scr[...].astype(jnp.bfloat16)
            stat_ref[0, hl : hl + 1, qs] = seg_max
            stat_ref[0, head_share + hl : head_share + hl + 1, qs] = total_scr[...]


def local_attention(queries, keys, values, block_list, block_count, first_block, shards):
    rows = queries.shape[0]
    ctx_span = keys.shape[0]
    head_share = HEADS // shards
    share_width = head_share * HEAD_DIM
    q_blocks = rows // BLOCK
    k_blocks = ctx_span // BLOCK
    max_sel = block_list.shape[1]
    shape = (rows, head_share, q_blocks, k_blocks, max_sel)
    grid_spec = pltpu.PrefetchScalarGridSpec(
        num_scalar_prefetch=3,
        grid=(shards,),
        in_specs=[
            pl.BlockSpec((rows, share_width), lambda g, *_: (0, g)),
            pl.BlockSpec((ctx_span, share_width), lambda g, *_: (0, g)),
            pl.BlockSpec((ctx_span, share_width), lambda g, *_: (0, g)),
        ],
        out_specs=[
            pl.BlockSpec((head_share, rows, HEAD_DIM), lambda g, *_: (g, 0, 0)),
            pl.BlockSpec((1, 2 * head_share, rows), lambda g, *_: (g, 0, 0)),
        ],
        scratch_shapes=[
            pltpu.SMEM((q_blocks * k_blocks,), jnp.int32),
            pltpu.VMEM((ctx_span, BLOCK), jnp.float32),
            pltpu.VMEM((1, BLOCK), jnp.float32),
            pltpu.VMEM((1, BLOCK), jnp.float32),
            pltpu.VMEM((BLOCK, HEAD_DIM), jnp.float32),
        ],
    )
    flops = 4 * HEADS * rows * ctx_span * HEAD_DIM
    return pl.pallas_call(
        functools.partial(attention_kernel, shape),
        grid_spec=grid_spec,
        out_shape=[
            jax.ShapeDtypeStruct((HEADS, rows, HEAD_DIM), jnp.bfloat16),
            jax.ShapeDtypeStruct((shards, 2 * head_share, rows), jnp.float32),
        ],
        compiler_params=pltpu.CompilerParams(dimension_semantics=("arbitrary",)),
        cost_estimate=pl.CostEstimate(
            flops=flops,
            transcendentals=HEADS * rows * ctx_span,
            bytes_accessed=2 * (queries.size + keys.size + values.size) + 2 * rows * HEADS * HEAD_DIM,
        ),
    )(block_list, block_count, first_block, queries, keys, values)


def split_three(x):
    hi = lax.reduce_precision(x, exponent_bits=8, mantissa_bits=7)
    rest = x - hi
    mid = lax.reduce_precision(rest, exponent_bits=8, mantissa_bits=7)
    lo = lax.reduce_precision(rest - mid, exponent_bits=8, mantissa_bits=7)
    return jnp.stack([hi, mid, lo], axis=1).astype(jnp.bfloat16)


def join_three(parts):
    parts = parts.astype(jnp.float32)
    return (parts[:, 0] + parts[:, 1]) + parts[:, 2]


def local(queries, keys, values, block_list, block_count):
    row_count = queries.shape[0]
    ctx_span = keys.shape[0]
    shards = lax.axis_size("ctx")
    owners = lax.axis_size("row")
    per_owner = row_count // owners
    head_share = HEADS // shards
    share_width = head_share * HEAD_DIM
    blocks_here = ctx_span // BLOCK
    first_block = (lax.axis_index("ctx") * blocks_here).astype(jnp.int32).reshape(1)
    part, stat = local_attention(
        queries, keys, values, block_list.astype(jnp.int32), block_count.astype(jnp.int32), first_block, shards
    )
    part_low = part.reshape(shards, head_share, per_owner, owners, HEAD_DIM)
    part_low = jnp.transpose(part_low, (3, 0, 1, 2, 4)).reshape(
        owners * shards, head_share * per_owner, HEAD_DIM
    )
    stats = jnp.transpose(stat.reshape(shards, 2, head_share, per_owner, owners), (4, 0, 1, 2, 3))
    stats = stats.reshape(owners * shards, 2, head_share, per_owner)
    stat_count = 3 * 2 * head_share * per_owner
    stat_rows = -(-stat_count // HEAD_DIM)
    stat_low = split_three(stats).reshape(owners * shards, stat_count)
    stat_low = jnp.pad(stat_low, ((0, 0), (0, stat_rows * HEAD_DIM - stat_count)))
    payload = jnp.concatenate(
        [part_low, stat_low.reshape(owners * shards, stat_rows, HEAD_DIM)], axis=1
    )
    arrived = lax.all_to_all(payload, ("row", "ctx"), 0, 0, tiled=True)
    arrived = arrived.reshape(owners, shards, head_share * per_owner + stat_rows, HEAD_DIM)
    part_in = arrived[:, :, : head_share * per_owner].reshape(owners, shards, head_share, per_owner, HEAD_DIM)
    stat_in = arrived[:, :, head_share * per_owner :].reshape(owners * shards, stat_rows * HEAD_DIM)
    stats_in = join_three(
        stat_in[:, :stat_count].reshape(owners * shards, 3, 2, head_share, per_owner)
    ).reshape(owners, shards, 2, head_share, per_owner)
    maxima = stats_in[:, :, 0]
    totals = stats_in[:, :, 1]
    row_best = jnp.max(maxima, axis=1)
    weight = jnp.exp(maxima - row_best[:, None])
    total_sum = jnp.sum(totals * weight, axis=1)
    numerator = jnp.sum(part_in.astype(jnp.float32) * weight[..., None], axis=1)
    attended = numerator / total_sum[..., None]
    attended_low = jnp.transpose(attended, (0, 2, 1, 3)).reshape(row_count, share_width)
    return attended_low.astype(jnp.bfloat16)


def solution(mesh):
    return jax.shard_map(
        local,
        mesh=mesh,
        in_specs=(P("row", None), P("ctx", None), P("ctx", None), P("row", None), P("row")),
        out_specs=P("row", "ctx"),
        check_vma=False,
    )
```

```python
import functools

import jax
import jax.numpy as jnp
from jax import lax
from jax.experimental import pallas as pl
from jax.experimental.pallas import tpu as pltpu
from jax.sharding import PartitionSpec as P

HEADS = 16
HEAD_DIM = 128
BLOCK = 128


masked_fill = -1e30


def attention_kernel(shape, list_ref, count_ref, first_ref, q_ref, k_ref, v_ref, part_ref, stat_ref,
                     bias_ref, dead_ref):
    rows, head_share, q_blocks, k_blocks, max_sel = shape

    @pl.when(pl.program_id(0) == 0)
    def _():
        first = first_ref[0]
        for a in range(q_blocks):
            any_live = jnp.int32(0)
            for b in range(k_blocks):
                hit = jnp.int32(0)
                for slot in range(max_sel):
                    found = (list_ref[a, slot] == first + b) & (slot < count_ref[a])
                    hit = jnp.maximum(hit, jnp.where(found, 1, 0).astype(jnp.int32))
                any_live = jnp.maximum(any_live, hit)
                bias = jnp.where(hit > 0, 0.0, masked_fill).astype(jnp.float32)
                bias_ref[b * BLOCK : (b + 1) * BLOCK, a * BLOCK : (a + 1) * BLOCK] = jnp.full(
                    (BLOCK, BLOCK), bias, jnp.float32
                )
            dead = jnp.where(any_live > 0, 0.0, jnp.inf).astype(jnp.float32)
            dead_ref[:, a * BLOCK : (a + 1) * BLOCK] = jnp.full((8, BLOCK), dead, jnp.float32)

    score_scale = 1.0 / HEAD_DIM**0.5
    dead_row = dead_ref[0:1, :]
    for hl in range(head_share):
        cols = slice(hl * HEAD_DIM, (hl + 1) * HEAD_DIM)
        scores = lax.dot_general(
            k_ref[:, cols], q_ref[:, cols], (((1,), (1,)), ((), ())), preferred_element_type=jnp.float32
        )
        scores = scores * score_scale + bias_ref[...]
        seg_max = jnp.max(scores, axis=0, keepdims=True)
        probs = jnp.exp(scores - (seg_max + dead_row))
        seg_total = jnp.sum(probs, axis=0, keepdims=True)
        seg_out = lax.dot_general(
            probs.astype(jnp.bfloat16), v_ref[:, cols], (((0,), (0,)), ((), ())),
            preferred_element_type=jnp.float32,
        )
        part_ref[hl] = seg_out
        stat_ref[0, hl : hl + 1, :] = seg_max
        stat_ref[0, head_share + hl : head_share + hl + 1, :] = seg_total


def local_attention(queries, keys, values, block_list, block_count, first_block, shards):
    rows = queries.shape[0]
    ctx_span = keys.shape[0]
    head_share = HEADS // shards
    share_width = head_share * HEAD_DIM
    q_blocks = rows // BLOCK
    k_blocks = ctx_span // BLOCK
    max_sel = block_list.shape[1]
    shape = (rows, head_share, q_blocks, k_blocks, max_sel)
    grid_spec = pltpu.PrefetchScalarGridSpec(
        num_scalar_prefetch=3,
        grid=(shards,),
        in_specs=[
            pl.BlockSpec((rows, share_width), lambda g, *_: (0, g)),
            pl.BlockSpec((ctx_span, share_width), lambda g, *_: (0, g)),
            pl.BlockSpec((ctx_span, share_width), lambda g, *_: (0, g)),
        ],
        out_specs=[
            pl.BlockSpec((head_share, rows, HEAD_DIM), lambda g, *_: (g, 0, 0)),
            pl.BlockSpec((1, 2 * head_share, rows), lambda g, *_: (g, 0, 0)),
        ],
        scratch_shapes=[
            pltpu.VMEM((ctx_span, rows), jnp.float32),
            pltpu.VMEM((8, rows), jnp.float32),
        ],
    )
    flops = 4 * HEADS * rows * ctx_span * HEAD_DIM
    return pl.pallas_call(
        functools.partial(attention_kernel, shape),
        grid_spec=grid_spec,
        out_shape=[
            jax.ShapeDtypeStruct((HEADS, rows, HEAD_DIM), jnp.float32),
            jax.ShapeDtypeStruct((shards, 2 * head_share, rows), jnp.float32),
        ],
        compiler_params=pltpu.CompilerParams(dimension_semantics=("arbitrary",)),
        cost_estimate=pl.CostEstimate(
            flops=flops,
            transcendentals=HEADS * rows * ctx_span,
            bytes_accessed=2 * (queries.size + keys.size + values.size) + 2 * rows * HEADS * HEAD_DIM,
        ),
    )(block_list, block_count, first_block, queries, keys, values)


def split_three(x):
    hi = lax.reduce_precision(x, exponent_bits=8, mantissa_bits=7)
    rest = x - hi
    mid = lax.reduce_precision(rest, exponent_bits=8, mantissa_bits=7)
    lo = lax.reduce_precision(rest - mid, exponent_bits=8, mantissa_bits=7)
    return jnp.stack([hi, mid, lo], axis=1).astype(jnp.bfloat16)


def join_three(parts):
    parts = parts.astype(jnp.float32)
    return (parts[:, 0] + parts[:, 1]) + parts[:, 2]


def local(queries, keys, values, block_list, block_count):
    row_count = queries.shape[0]
    ctx_span = keys.shape[0]
    shards = lax.axis_size("ctx")
    owners = lax.axis_size("row")
    per_owner = row_count // owners
    head_share = HEADS // shards
    share_width = head_share * HEAD_DIM
    blocks_here = ctx_span // BLOCK
    first_block = (lax.axis_index("ctx") * blocks_here).astype(jnp.int32).reshape(1)
    part, stat = local_attention(
        queries, keys, values, block_list.astype(jnp.int32), block_count.astype(jnp.int32), first_block, shards
    )
    part_low = part.reshape(shards, head_share, per_owner, owners, HEAD_DIM)
    part_low = jnp.transpose(part_low, (3, 0, 1, 2, 4)).reshape(
        owners * shards, head_share * per_owner, HEAD_DIM
    ).astype(jnp.bfloat16)
    stats = jnp.transpose(stat.reshape(shards, 2, head_share, per_owner, owners), (4, 0, 1, 2, 3))
    stats = stats.reshape(owners * shards, 2, head_share, per_owner)
    stat_count = 3 * 2 * head_share * per_owner
    stat_rows = -(-stat_count // HEAD_DIM)
    stat_low = split_three(stats).reshape(owners * shards, stat_count)
    stat_low = jnp.pad(stat_low, ((0, 0), (0, stat_rows * HEAD_DIM - stat_count)))
    payload = jnp.concatenate(
        [part_low, stat_low.reshape(owners * shards, stat_rows, HEAD_DIM)], axis=1
    )
    arrived = lax.all_to_all(payload, ("row", "ctx"), 0, 0, tiled=True)
    arrived = arrived.reshape(owners, shards, head_share * per_owner + stat_rows, HEAD_DIM)
    part_in = arrived[:, :, : head_share * per_owner].reshape(owners, shards, head_share, per_owner, HEAD_DIM)
    stat_in = arrived[:, :, head_share * per_owner :].reshape(owners * shards, stat_rows * HEAD_DIM)
    stats_in = join_three(
        stat_in[:, :stat_count].reshape(owners * shards, 3, 2, head_share, per_owner)
    ).reshape(owners, shards, 2, head_share, per_owner)
    maxima = stats_in[:, :, 0]
    totals = stats_in[:, :, 1]
    row_best = jnp.max(maxima, axis=1)
    weight = jnp.exp(maxima - row_best[:, None])
    total_sum = jnp.sum(totals * weight, axis=1)
    numerator = jnp.sum(part_in.astype(jnp.float32) * weight[..., None], axis=1)
    attended = numerator / total_sum[..., None]
    attended_low = jnp.transpose(attended, (0, 2, 1, 3)).reshape(row_count, share_width)
    return attended_low.astype(jnp.bfloat16)


def solution(mesh):
    return jax.shard_map(
        local,
        mesh=mesh,
        in_specs=(P("row", None), P("ctx", None), P("ctx", None), P("row", None), P("row")),
        out_specs=P("row", "ctx"),
        check_vma=False,
    )
```

```python
import functools

import jax
import jax.numpy as jnp
from jax import lax
from jax.experimental import pallas as pl
from jax.experimental.pallas import tpu as pltpu
from jax.sharding import PartitionSpec as P

HEADS = 16
HEAD_DIM = 128
BLOCK = 128
HEADS_PER_STEP = 8


masked_fill = -1e30


def attention_kernel(shape, list_ref, count_ref, first_ref, q_ref, k_ref, v_ref, part_ref, stat_ref,
                     bias_ref, dead_ref):
    rows, head_share, q_blocks, k_blocks, max_sel = shape

    @pl.when(pl.program_id(0) == 0)
    def _():
        first = first_ref[0]
        for a in range(q_blocks):
            any_live = jnp.int32(0)
            for b in range(k_blocks):
                hit = jnp.int32(0)
                for slot in range(max_sel):
                    found = (list_ref[a, slot] == first + b) & (slot < count_ref[a])
                    hit = jnp.maximum(hit, jnp.where(found, 1, 0).astype(jnp.int32))
                any_live = jnp.maximum(any_live, hit)
                bias = jnp.where(hit > 0, 0.0, masked_fill).astype(jnp.float32)
                bias_ref[b * BLOCK : (b + 1) * BLOCK, a * BLOCK : (a + 1) * BLOCK] = jnp.full(
                    (BLOCK, BLOCK), bias, jnp.float32
                )
            dead = jnp.where(any_live > 0, 0.0, jnp.inf).astype(jnp.float32)
            dead_ref[:, a * BLOCK : (a + 1) * BLOCK] = jnp.full((8, BLOCK), dead, jnp.float32)

    score_scale = 1.0 / HEAD_DIM**0.5
    dead_row = dead_ref[0:1, :]
    for hl in range(head_share):
        cols = slice(hl * HEAD_DIM, (hl + 1) * HEAD_DIM)
        scores = lax.dot_general(
            k_ref[:, cols], q_ref[:, cols], (((1,), (1,)), ((), ())), preferred_element_type=jnp.float32
        )
        scores = scores * score_scale + bias_ref[...]
        seg_max = jnp.max(scores, axis=0, keepdims=True)
        probs = jnp.exp(scores - (seg_max + dead_row))
        seg_total = jnp.sum(probs, axis=0, keepdims=True)
        seg_out = lax.dot_general(
            probs.astype(jnp.bfloat16), v_ref[:, cols], (((0,), (0,)), ((), ())),
            preferred_element_type=jnp.float32,
        )
        part_ref[hl] = seg_out.astype(jnp.bfloat16)
        stat_ref[0, hl : hl + 1, :] = seg_max
        stat_ref[1, hl : hl + 1, :] = seg_total


def local_attention(queries, keys, values, block_list, block_count, first_block, shards):
    rows = queries.shape[0]
    ctx_span = keys.shape[0]
    step_heads = HEADS_PER_STEP
    step_width = step_heads * HEAD_DIM
    q_blocks = rows // BLOCK
    k_blocks = ctx_span // BLOCK
    max_sel = block_list.shape[1]
    shape = (rows, step_heads, q_blocks, k_blocks, max_sel)
    grid_spec = pltpu.PrefetchScalarGridSpec(
        num_scalar_prefetch=3,
        grid=(HEADS // step_heads,),
        in_specs=[
            pl.BlockSpec((rows, step_width), lambda g, *_: (0, g)),
            pl.BlockSpec((ctx_span, step_width), lambda g, *_: (0, g)),
            pl.BlockSpec((ctx_span, step_width), lambda g, *_: (0, g)),
        ],
        out_specs=[
            pl.BlockSpec((step_heads, rows, HEAD_DIM), lambda g, *_: (g, 0, 0)),
            pl.BlockSpec((2, step_heads, rows), lambda g, *_: (0, g, 0)),
        ],
        scratch_shapes=[
            pltpu.VMEM((ctx_span, rows), jnp.float32),
            pltpu.VMEM((8, rows), jnp.float32),
        ],
    )
    flops = 4 * HEADS * rows * ctx_span * HEAD_DIM
    return pl.pallas_call(
        functools.partial(attention_kernel, shape),
        grid_spec=grid_spec,
        out_shape=[
            jax.ShapeDtypeStruct((HEADS, rows, HEAD_DIM), jnp.bfloat16),
            jax.ShapeDtypeStruct((2, HEADS, rows), jnp.float32),
        ],
        compiler_params=pltpu.CompilerParams(dimension_semantics=("arbitrary",)),
        cost_estimate=pl.CostEstimate(
            flops=flops,
            transcendentals=HEADS * rows * ctx_span,
            bytes_accessed=2 * (queries.size + keys.size + values.size) + 2 * rows * HEADS * HEAD_DIM,
        ),
    )(block_list, block_count, first_block, queries, keys, values)


def split_three(x):
    hi = lax.reduce_precision(x, exponent_bits=8, mantissa_bits=7)
    rest = x - hi
    mid = lax.reduce_precision(rest, exponent_bits=8, mantissa_bits=7)
    lo = lax.reduce_precision(rest - mid, exponent_bits=8, mantissa_bits=7)
    return jnp.stack([hi, mid, lo], axis=1).astype(jnp.bfloat16)


def join_three(parts):
    parts = parts.astype(jnp.float32)
    return (parts[:, 0] + parts[:, 1]) + parts[:, 2]


def local(queries, keys, values, block_list, block_count):
    row_count = queries.shape[0]
    ctx_span = keys.shape[0]
    shards = lax.axis_size("ctx")
    owners = lax.axis_size("row")
    per_owner = row_count // owners
    head_share = HEADS // shards
    share_width = head_share * HEAD_DIM
    blocks_here = ctx_span // BLOCK
    first_block = (lax.axis_index("ctx") * blocks_here).astype(jnp.int32).reshape(1)
    part, stat = local_attention(
        queries, keys, values, block_list.astype(jnp.int32), block_count.astype(jnp.int32), first_block, shards
    )
    part_low = part.reshape(shards, head_share, per_owner, owners, HEAD_DIM)
    part_low = jnp.transpose(part_low, (3, 0, 1, 2, 4)).reshape(
        owners * shards, head_share * per_owner, HEAD_DIM
    )
    stats = jnp.transpose(stat.reshape(2, shards, head_share, per_owner, owners), (4, 1, 0, 2, 3))
    stats = stats.reshape(owners * shards, 2, head_share, per_owner)
    stat_count = 3 * 2 * head_share * per_owner
    stat_rows = -(-stat_count // HEAD_DIM)
    stat_low = split_three(stats).reshape(owners * shards, stat_count)
    stat_low = jnp.pad(stat_low, ((0, 0), (0, stat_rows * HEAD_DIM - stat_count)))
    payload = jnp.concatenate(
        [part_low, stat_low.reshape(owners * shards, stat_rows, HEAD_DIM)], axis=1
    )
    arrived = lax.all_to_all(payload, ("row", "ctx"), 0, 0, tiled=True)
    arrived = arrived.reshape(owners, shards, head_share * per_owner + stat_rows, HEAD_DIM)
    part_in = arrived[:, :, : head_share * per_owner].reshape(owners, shards, head_share, per_owner, HEAD_DIM)
    stat_in = arrived[:, :, head_share * per_owner :].reshape(owners * shards, stat_rows * HEAD_DIM)
    stats_in = join_three(
        stat_in[:, :stat_count].reshape(owners * shards, 3, 2, head_share, per_owner)
    ).reshape(owners, shards, 2, head_share, per_owner)
    maxima = stats_in[:, :, 0]
    totals = stats_in[:, :, 1]
    row_best = jnp.max(maxima, axis=1)
    weight = jnp.exp(maxima - row_best[:, None])
    total_sum = jnp.sum(totals * weight, axis=1)
    numerator = jnp.sum(part_in.astype(jnp.float32) * weight[..., None], axis=1)
    attended = numerator / total_sum[..., None]
    attended_low = jnp.transpose(attended, (0, 2, 1, 3)).reshape(row_count, share_width)
    return attended_low.astype(jnp.bfloat16)


def solution(mesh):
    return jax.shard_map(
        local,
        mesh=mesh,
        in_specs=(P("row", None), P("ctx", None), P("ctx", None), P("row", None), P("row")),
        out_specs=P("row", "ctx"),
        check_vma=False,
    )
```

```python
import functools

import jax
import jax.numpy as jnp
from jax import lax
from jax.experimental import pallas as pl
from jax.experimental.pallas import tpu as pltpu
from jax.sharding import PartitionSpec as P

HEADS = 16
HEAD_DIM = 128
BLOCK = 128
HEADS_PER_STEP = 16


masked_fill = -1e30


def attention_kernel(shape, list_ref, count_ref, first_ref, q_ref, k_ref, v_ref, part_ref, stat_ref,
                     bias_ref, dead_ref):
    rows, head_share, q_blocks, k_blocks, max_sel = shape

    @pl.when(pl.program_id(0) == 0)
    def _():
        first = first_ref[0]
        for a in range(q_blocks):
            any_live = jnp.int32(0)
            for b in range(k_blocks):
                hit = jnp.int32(0)
                for slot in range(max_sel):
                    found = (list_ref[a, slot] == first + b) & (slot < count_ref[a])
                    hit = jnp.maximum(hit, jnp.where(found, 1, 0).astype(jnp.int32))
                any_live = jnp.maximum(any_live, hit)
                bias = jnp.where(hit > 0, 0.0, masked_fill).astype(jnp.float32)
                bias_ref[b * BLOCK : (b + 1) * BLOCK, a * BLOCK : (a + 1) * BLOCK] = jnp.full(
                    (BLOCK, BLOCK), bias, jnp.float32
                )
            dead = jnp.where(any_live > 0, 0.0, jnp.inf).astype(jnp.float32)
            dead_ref[:, a * BLOCK : (a + 1) * BLOCK] = jnp.full((8, BLOCK), dead, jnp.float32)

    score_scale = 1.0 / HEAD_DIM**0.5
    dead_row = dead_ref[0:1, :]
    for hl in range(head_share):
        cols = slice(hl * HEAD_DIM, (hl + 1) * HEAD_DIM)
        scores = lax.dot_general(
            k_ref[:, cols], q_ref[:, cols], (((1,), (1,)), ((), ())), preferred_element_type=jnp.float32
        )
        scores = scores * score_scale + bias_ref[...]
        seg_max = jnp.max(scores, axis=0, keepdims=True)
        probs = jnp.exp(scores - (seg_max + dead_row))
        seg_total = jnp.sum(probs, axis=0, keepdims=True)
        seg_out = lax.dot_general(
            probs.astype(jnp.bfloat16), v_ref[:, cols], (((0,), (0,)), ((), ())),
            preferred_element_type=jnp.float32,
        )
        part_ref[hl] = seg_out.astype(jnp.bfloat16)
        stat_ref[0, hl : hl + 1, :] = seg_max
        stat_ref[1, hl : hl + 1, :] = seg_total


def local_attention(queries, keys, values, block_list, block_count, first_block, shards):
    rows = queries.shape[0]
    ctx_span = keys.shape[0]
    step_heads = HEADS_PER_STEP
    step_width = step_heads * HEAD_DIM
    q_blocks = rows // BLOCK
    k_blocks = ctx_span // BLOCK
    max_sel = block_list.shape[1]
    shape = (rows, step_heads, q_blocks, k_blocks, max_sel)
    grid_spec = pltpu.PrefetchScalarGridSpec(
        num_scalar_prefetch=3,
        grid=(HEADS // step_heads,),
        in_specs=[
            pl.BlockSpec((rows, step_width), lambda g, *_: (0, g)),
            pl.BlockSpec((ctx_span, step_width), lambda g, *_: (0, g)),
            pl.BlockSpec((ctx_span, step_width), lambda g, *_: (0, g)),
        ],
        out_specs=[
            pl.BlockSpec((step_heads, rows, HEAD_DIM), lambda g, *_: (g, 0, 0)),
            pl.BlockSpec((2, step_heads, rows), lambda g, *_: (0, g, 0)),
        ],
        scratch_shapes=[
            pltpu.VMEM((ctx_span, rows), jnp.float32),
            pltpu.VMEM((8, rows), jnp.float32),
        ],
    )
    flops = 4 * HEADS * rows * ctx_span * HEAD_DIM
    return pl.pallas_call(
        functools.partial(attention_kernel, shape),
        grid_spec=grid_spec,
        out_shape=[
            jax.ShapeDtypeStruct((HEADS, rows, HEAD_DIM), jnp.bfloat16),
            jax.ShapeDtypeStruct((2, HEADS, rows), jnp.float32),
        ],
        compiler_params=pltpu.CompilerParams(dimension_semantics=("arbitrary",)),
        cost_estimate=pl.CostEstimate(
            flops=flops,
            transcendentals=HEADS * rows * ctx_span,
            bytes_accessed=2 * (queries.size + keys.size + values.size) + 2 * rows * HEADS * HEAD_DIM,
        ),
    )(block_list, block_count, first_block, queries, keys, values)


def split_three(x):
    hi = lax.reduce_precision(x, exponent_bits=8, mantissa_bits=7)
    rest = x - hi
    mid = lax.reduce_precision(rest, exponent_bits=8, mantissa_bits=7)
    lo = lax.reduce_precision(rest - mid, exponent_bits=8, mantissa_bits=7)
    return jnp.stack([hi, mid, lo], axis=1).astype(jnp.bfloat16)


def join_three(parts):
    parts = parts.astype(jnp.float32)
    return (parts[:, 0] + parts[:, 1]) + parts[:, 2]


def local(queries, keys, values, block_list, block_count):
    row_count = queries.shape[0]
    ctx_span = keys.shape[0]
    shards = lax.axis_size("ctx")
    owners = lax.axis_size("row")
    per_owner = row_count // owners
    head_share = HEADS // shards
    share_width = head_share * HEAD_DIM
    blocks_here = ctx_span // BLOCK
    first_block = (lax.axis_index("ctx") * blocks_here).astype(jnp.int32).reshape(1)
    part, stat = local_attention(
        queries, keys, values, block_list.astype(jnp.int32), block_count.astype(jnp.int32), first_block, shards
    )
    part_low = part.reshape(shards, head_share, per_owner, owners, HEAD_DIM)
    part_low = jnp.transpose(part_low, (3, 0, 1, 2, 4)).reshape(
        owners * shards, head_share * per_owner, HEAD_DIM
    )
    stats = jnp.transpose(stat.reshape(2, shards, head_share, per_owner, owners), (4, 1, 0, 2, 3))
    stats = stats.reshape(owners * shards, 2, head_share, per_owner)
    stat_count = 3 * 2 * head_share * per_owner
    stat_rows = -(-stat_count // HEAD_DIM)
    stat_low = split_three(stats).reshape(owners * shards, stat_count)
    stat_low = jnp.pad(stat_low, ((0, 0), (0, stat_rows * HEAD_DIM - stat_count)))
    payload = jnp.concatenate(
        [part_low, stat_low.reshape(owners * shards, stat_rows, HEAD_DIM)], axis=1
    )
    arrived = lax.all_to_all(payload, ("row", "ctx"), 0, 0, tiled=True)
    arrived = arrived.reshape(owners, shards, head_share * per_owner + stat_rows, HEAD_DIM)
    part_in = arrived[:, :, : head_share * per_owner].reshape(owners, shards, head_share, per_owner, HEAD_DIM)
    stat_in = arrived[:, :, head_share * per_owner :].reshape(owners * shards, stat_rows * HEAD_DIM)
    stats_in = join_three(
        stat_in[:, :stat_count].reshape(owners * shards, 3, 2, head_share, per_owner)
    ).reshape(owners, shards, 2, head_share, per_owner)
    maxima = stats_in[:, :, 0]
    totals = stats_in[:, :, 1]
    row_best = jnp.max(maxima, axis=1)
    weight = jnp.exp(maxima - row_best[:, None])
    total_sum = jnp.sum(totals * weight, axis=1)
    numerator = jnp.sum(part_in.astype(jnp.float32) * weight[..., None], axis=1)
    attended = numerator / total_sum[..., None]
    attended_low = jnp.transpose(attended, (0, 2, 1, 3)).reshape(row_count, share_width)
    return attended_low.astype(jnp.bfloat16)


def solution(mesh):
    return jax.shard_map(
        local,
        mesh=mesh,
        in_specs=(P("row", None), P("ctx", None), P("ctx", None), P("row", None), P("row")),
        out_specs=P("row", "ctx"),
        check_vma=False,
    )
```

```python
import functools

import jax
import jax.numpy as jnp
from jax import lax
from jax.experimental import pallas as pl
from jax.experimental.pallas import tpu as pltpu
from jax.sharding import PartitionSpec as P

HEADS = 16
HEAD_DIM = 128
BLOCK = 128
HEADS_PER_STEP = 16


masked_fill = -1e30


def attention_kernel(shape, list_ref, count_ref, first_ref, q_ref, k_ref, v_ref, part_ref, stat_ref,
                     bias_ref, dead_ref):
    rows, head_share, q_blocks, k_blocks, max_sel = shape

    @pl.when(pl.program_id(0) == 0)
    def _():
        first = first_ref[0]
        for a in range(q_blocks):
            any_live = jnp.int32(0)
            for b in range(k_blocks):
                hit = jnp.int32(0)
                for slot in range(max_sel):
                    found = (list_ref[a, slot] == first + b) & (slot < count_ref[a])
                    hit = jnp.maximum(hit, jnp.where(found, 1, 0).astype(jnp.int32))
                any_live = jnp.maximum(any_live, hit)
                bias = jnp.where(hit > 0, 0.0, masked_fill).astype(jnp.float32)
                bias_ref[b * BLOCK : (b + 1) * BLOCK, a * BLOCK : (a + 1) * BLOCK] = jnp.full(
                    (BLOCK, BLOCK), bias, jnp.float32
                )
            dead = jnp.where(any_live > 0, 0.0, jnp.inf).astype(jnp.float32)
            dead_ref[:, a * BLOCK : (a + 1) * BLOCK] = jnp.full((8, BLOCK), dead, jnp.float32)

    score_scale = 1.0 / HEAD_DIM**0.5
    dead_row = dead_ref[0:1, :]
    for hl in range(head_share):
        cols = slice(hl * HEAD_DIM, (hl + 1) * HEAD_DIM)
        scores = lax.dot_general(
            k_ref[:, cols], q_ref[:, cols], (((1,), (1,)), ((), ())), preferred_element_type=jnp.float32
        )
        scores = scores * score_scale + bias_ref[...]
        seg_max = jnp.max(scores, axis=0, keepdims=True)
        probs = jnp.exp(scores - (seg_max + dead_row))
        seg_total = jnp.sum(probs, axis=0, keepdims=True)
        seg_out = lax.dot_general(
            probs.astype(jnp.bfloat16), v_ref[:, cols], (((0,), (0,)), ((), ())),
            preferred_element_type=jnp.float32,
        )
        part_ref[hl] = seg_out.astype(jnp.bfloat16)
        for kind, value in enumerate((seg_max, seg_total)):
            hi = value.astype(jnp.bfloat16)
            rest = value - hi.astype(jnp.float32)
            mid = rest.astype(jnp.bfloat16)
            lo = (rest - mid.astype(jnp.float32)).astype(jnp.bfloat16)
            for part, piece in enumerate((hi, mid, lo)):
                stat_ref[part, kind, hl : hl + 1, :] = piece


def local_attention(queries, keys, values, block_list, block_count, first_block, shards):
    rows = queries.shape[0]
    ctx_span = keys.shape[0]
    step_heads = HEADS_PER_STEP
    step_width = step_heads * HEAD_DIM
    q_blocks = rows // BLOCK
    k_blocks = ctx_span // BLOCK
    max_sel = block_list.shape[1]
    shape = (rows, step_heads, q_blocks, k_blocks, max_sel)
    grid_spec = pltpu.PrefetchScalarGridSpec(
        num_scalar_prefetch=3,
        grid=(HEADS // step_heads,),
        in_specs=[
            pl.BlockSpec((rows, step_width), lambda g, *_: (0, g)),
            pl.BlockSpec((ctx_span, step_width), lambda g, *_: (0, g)),
            pl.BlockSpec((ctx_span, step_width), lambda g, *_: (0, g)),
        ],
        out_specs=[
            pl.BlockSpec((step_heads, rows, HEAD_DIM), lambda g, *_: (g, 0, 0)),
            pl.BlockSpec((3, 2, step_heads, rows), lambda g, *_: (0, 0, g, 0)),
        ],
        scratch_shapes=[
            pltpu.VMEM((ctx_span, rows), jnp.float32),
            pltpu.VMEM((8, rows), jnp.float32),
        ],
    )
    flops = 4 * HEADS * rows * ctx_span * HEAD_DIM
    return pl.pallas_call(
        functools.partial(attention_kernel, shape),
        grid_spec=grid_spec,
        out_shape=[
            jax.ShapeDtypeStruct((HEADS, rows, HEAD_DIM), jnp.bfloat16),
            jax.ShapeDtypeStruct((3, 2, HEADS, rows), jnp.bfloat16),
        ],
        compiler_params=pltpu.CompilerParams(dimension_semantics=("arbitrary",)),
        cost_estimate=pl.CostEstimate(
            flops=flops,
            transcendentals=HEADS * rows * ctx_span,
            bytes_accessed=2 * (queries.size + keys.size + values.size) + 2 * rows * HEADS * HEAD_DIM,
        ),
    )(block_list, block_count, first_block, queries, keys, values)


def split_three(x):
    hi = lax.reduce_precision(x, exponent_bits=8, mantissa_bits=7)
    rest = x - hi
    mid = lax.reduce_precision(rest, exponent_bits=8, mantissa_bits=7)
    lo = lax.reduce_precision(rest - mid, exponent_bits=8, mantissa_bits=7)
    return jnp.stack([hi, mid, lo], axis=1).astype(jnp.bfloat16)


def join_three(parts):
    parts = parts.astype(jnp.float32)
    return (parts[:, 0] + parts[:, 1]) + parts[:, 2]


def local(queries, keys, values, block_list, block_count):
    row_count = queries.shape[0]
    ctx_span = keys.shape[0]
    shards = lax.axis_size("ctx")
    owners = lax.axis_size("row")
    per_owner = row_count // owners
    head_share = HEADS // shards
    share_width = head_share * HEAD_DIM
    blocks_here = ctx_span // BLOCK
    first_block = (lax.axis_index("ctx") * blocks_here).astype(jnp.int32).reshape(1)
    part, stat = local_attention(
        queries, keys, values, block_list.astype(jnp.int32), block_count.astype(jnp.int32), first_block, shards
    )
    part_low = part.reshape(shards, head_share, per_owner, owners, HEAD_DIM)
    part_low = jnp.transpose(part_low, (3, 0, 1, 2, 4)).reshape(
        owners * shards, head_share * per_owner, HEAD_DIM
    )
    stats = jnp.transpose(stat.reshape(3, 2, shards, head_share, per_owner, owners), (5, 2, 0, 1, 3, 4))
    stat_count = 3 * 2 * head_share * per_owner
    stat_rows = -(-stat_count // HEAD_DIM)
    stat_low = stats.reshape(owners * shards, stat_count)
    stat_low = jnp.pad(stat_low, ((0, 0), (0, stat_rows * HEAD_DIM - stat_count)))
    payload = jnp.concatenate(
        [part_low, stat_low.reshape(owners * shards, stat_rows, HEAD_DIM)], axis=1
    )
    arrived = lax.all_to_all(payload, ("row", "ctx"), 0, 0, tiled=True)
    arrived = arrived.reshape(owners, shards, head_share * per_owner + stat_rows, HEAD_DIM)
    part_in = arrived[:, :, : head_share * per_owner].reshape(owners, shards, head_share, per_owner, HEAD_DIM)
    stat_in = arrived[:, :, head_share * per_owner :].reshape(owners * shards, stat_rows * HEAD_DIM)
    stats_in = join_three(
        stat_in[:, :stat_count].reshape(owners * shards, 3, 2, head_share, per_owner)
    ).reshape(owners, shards, 2, head_share, per_owner)
    maxima = stats_in[:, :, 0]
    totals = stats_in[:, :, 1]
    row_best = jnp.max(maxima, axis=1)
    weight = jnp.exp(maxima - row_best[:, None])
    total_sum = jnp.sum(totals * weight, axis=1)
    numerator = jnp.sum(part_in.astype(jnp.float32) * weight[..., None], axis=1)
    attended = numerator / total_sum[..., None]
    attended_low = jnp.transpose(attended, (0, 2, 1, 3)).reshape(row_count, share_width)
    return attended_low.astype(jnp.bfloat16)


def solution(mesh):
    return jax.shard_map(
        local,
        mesh=mesh,
        in_specs=(P("row", None), P("ctx", None), P("ctx", None), P("row", None), P("row")),
        out_specs=P("row", "ctx"),
        check_vma=False,
    )
```

```python
import functools

import jax
import jax.numpy as jnp
from jax import lax
from jax.experimental import pallas as pl
from jax.experimental.pallas import tpu as pltpu
from jax.sharding import PartitionSpec as P

HEADS = 16
HEAD_DIM = 128
BLOCK = 128
HEADS_PER_STEP = 16


masked_fill = -1e30


def attention_kernel(shape, list_ref, count_ref, first_ref, q_ref, k_ref, v_ref, part_ref, stat_ref,
                     bias_ref, dead_ref, q_scr):
    rows, owners, per_owner, head_share, q_blocks, k_blocks, max_sel = shape

    @pl.when(pl.program_id(0) == 0)
    def _():
        first = first_ref[0]
        pos = lax.broadcasted_iota(jnp.int32, (8, rows), 1)
        q_block = ((pos % per_owner) * owners + pos // per_owner) // BLOCK
        dead = jnp.full((8, rows), jnp.inf, jnp.float32)
        biases = [jnp.full((8, rows), masked_fill, jnp.float32) for _ in range(k_blocks)]
        for a in range(q_blocks):
            for b in range(k_blocks):
                hit = jnp.int32(0)
                for slot in range(max_sel):
                    found = (list_ref[a, slot] == first + b) & (slot < count_ref[a])
                    hit = jnp.maximum(hit, jnp.where(found, 1, 0).astype(jnp.int32))
                live = (q_block == a) & (hit > 0)
                biases[b] = jnp.where(live, 0.0, biases[b])
                dead = jnp.where(live, 0.0, dead)
        for b in range(k_blocks):
            bias_ref[b * BLOCK : (b + 1) * BLOCK, :] = jnp.broadcast_to(biases[b][0:1, :], (BLOCK, rows))
        dead_ref[...] = dead

    score_scale = 1.0 / HEAD_DIM**0.5
    dead_row = dead_ref[0:1, :]
    for hl in range(head_share):
        cols = slice(hl * HEAD_DIM, (hl + 1) * HEAD_DIM)
        q_scr[...] = q_ref[:, cols].astype(jnp.float32)
        q_perm = jnp.concatenate(
            [q_scr[pl.ds(r, per_owner, stride=owners), :] for r in range(owners)], axis=0
        ).astype(jnp.bfloat16)
        scores = lax.dot_general(
            k_ref[:, cols], q_perm, (((1,), (1,)), ((), ())), preferred_element_type=jnp.float32
        )
        scores = scores * score_scale + bias_ref[...]
        seg_max = jnp.max(scores, axis=0, keepdims=True)
        probs = jnp.exp(scores - (seg_max + dead_row))
        seg_total = jnp.sum(probs, axis=0, keepdims=True)
        seg_out = lax.dot_general(
            probs.astype(jnp.bfloat16), v_ref[:, cols], (((0,), (0,)), ((), ())),
            preferred_element_type=jnp.float32,
        )
        part_ref[hl] = seg_out.astype(jnp.bfloat16)
        stat_ref[0, hl : hl + 1, :] = seg_max
        stat_ref[1, hl : hl + 1, :] = seg_total


def local_attention(queries, keys, values, block_list, block_count, first_block, owners, shards):
    rows = queries.shape[0]
    per_owner = rows // owners
    ctx_span = keys.shape[0]
    step_heads = HEADS_PER_STEP
    step_width = step_heads * HEAD_DIM
    q_blocks = rows // BLOCK
    k_blocks = ctx_span // BLOCK
    max_sel = block_list.shape[1]
    shape = (rows, owners, per_owner, step_heads, q_blocks, k_blocks, max_sel)
    grid_spec = pltpu.PrefetchScalarGridSpec(
        num_scalar_prefetch=3,
        grid=(HEADS // step_heads,),
        in_specs=[
            pl.BlockSpec((rows, step_width), lambda g, *_: (0, g)),
            pl.BlockSpec((ctx_span, step_width), lambda g, *_: (0, g)),
            pl.BlockSpec((ctx_span, step_width), lambda g, *_: (0, g)),
        ],
        out_specs=[
            pl.BlockSpec((step_heads, rows, HEAD_DIM), lambda g, *_: (g, 0, 0)),
            pl.BlockSpec((2, step_heads, rows), lambda g, *_: (0, g, 0)),
        ],
        scratch_shapes=[
            pltpu.VMEM((ctx_span, rows), jnp.float32),
            pltpu.VMEM((8, rows), jnp.float32),
            pltpu.VMEM((rows, HEAD_DIM), jnp.float32),
        ],
    )
    flops = 4 * HEADS * rows * ctx_span * HEAD_DIM
    return pl.pallas_call(
        functools.partial(attention_kernel, shape),
        grid_spec=grid_spec,
        out_shape=[
            jax.ShapeDtypeStruct((HEADS, rows, HEAD_DIM), jnp.bfloat16),
            jax.ShapeDtypeStruct((2, HEADS, rows), jnp.float32),
        ],
        compiler_params=pltpu.CompilerParams(dimension_semantics=("arbitrary",)),
        cost_estimate=pl.CostEstimate(
            flops=flops,
            transcendentals=HEADS * rows * ctx_span,
            bytes_accessed=2 * (queries.size + keys.size + values.size) + 2 * rows * HEADS * HEAD_DIM,
        ),
    )(block_list, block_count, first_block, queries, keys, values)


def split_three(x):
    hi = lax.reduce_precision(x, exponent_bits=8, mantissa_bits=7)
    rest = x - hi
    mid = lax.reduce_precision(rest, exponent_bits=8, mantissa_bits=7)
    lo = lax.reduce_precision(rest - mid, exponent_bits=8, mantissa_bits=7)
    return jnp.stack([hi, mid, lo], axis=1).astype(jnp.bfloat16)


def join_three(parts):
    parts = parts.astype(jnp.float32)
    return (parts[:, 0] + parts[:, 1]) + parts[:, 2]


def local(queries, keys, values, block_list, block_count):
    row_count = queries.shape[0]
    ctx_span = keys.shape[0]
    shards = lax.axis_size("ctx")
    owners = lax.axis_size("row")
    per_owner = row_count // owners
    head_share = HEADS // shards
    share_width = head_share * HEAD_DIM
    blocks_here = ctx_span // BLOCK
    first_block = (lax.axis_index("ctx") * blocks_here).astype(jnp.int32).reshape(1)
    part, stat = local_attention(
        queries, keys, values, block_list.astype(jnp.int32), block_count.astype(jnp.int32), first_block, owners, shards
    )
    part_low = part.reshape(shards, head_share, owners, per_owner, HEAD_DIM)
    part_low = jnp.transpose(part_low, (2, 0, 1, 3, 4)).reshape(
        owners * shards, head_share * per_owner, HEAD_DIM
    )
    stats = jnp.transpose(stat.reshape(2, shards, head_share, owners, per_owner), (3, 1, 0, 2, 4))
    stats = stats.reshape(owners * shards, 2, head_share, per_owner)
    stat_count = 3 * 2 * head_share * per_owner
    stat_rows = -(-stat_count // HEAD_DIM)
    stat_low = split_three(stats).reshape(owners * shards, stat_count)
    stat_low = jnp.pad(stat_low, ((0, 0), (0, stat_rows * HEAD_DIM - stat_count)))
    payload = jnp.concatenate(
        [part_low, stat_low.reshape(owners * shards, stat_rows, HEAD_DIM)], axis=1
    )
    arrived = lax.all_to_all(payload, ("row", "ctx"), 0, 0, tiled=True)
    arrived = arrived.reshape(owners, shards, head_share * per_owner + stat_rows, HEAD_DIM)
    part_in = arrived[:, :, : head_share * per_owner].reshape(owners, shards, head_share, per_owner, HEAD_DIM)
    stat_in = arrived[:, :, head_share * per_owner :].reshape(owners * shards, stat_rows * HEAD_DIM)
    stats_in = join_three(
        stat_in[:, :stat_count].reshape(owners * shards, 3, 2, head_share, per_owner)
    ).reshape(owners, shards, 2, head_share, per_owner)
    maxima = stats_in[:, :, 0]
    totals = stats_in[:, :, 1]
    row_best = jnp.max(maxima, axis=1)
    weight = jnp.exp(maxima - row_best[:, None])
    total_sum = jnp.sum(totals * weight, axis=1)
    numerator = jnp.sum(part_in.astype(jnp.float32) * weight[..., None], axis=1)
    attended = numerator / total_sum[..., None]
    attended_low = jnp.transpose(attended, (0, 2, 1, 3)).reshape(row_count, share_width)
    return attended_low.astype(jnp.bfloat16)


def solution(mesh):
    return jax.shard_map(
        local,
        mesh=mesh,
        in_specs=(P("row", None), P("ctx", None), P("ctx", None), P("row", None), P("row")),
        out_specs=P("row", "ctx"),
        check_vma=False,
    )
```

```python
import functools

import jax
import jax.numpy as jnp
from jax import lax
from jax.experimental import pallas as pl
from jax.experimental.pallas import tpu as pltpu
from jax.sharding import PartitionSpec as P

HEADS = 16
HEAD_DIM = 128
BLOCK = 128
HEADS_PER_STEP = 16


masked_fill = -1e30


def attention_kernel(shape, list_ref, count_ref, first_ref, q_ref, k_ref, v_ref, part_ref, stat_ref,
                     bias_ref, dead_ref, q_scr):
    rows, owners, per_owner, head_share, q_blocks, k_blocks, max_sel = shape

    @pl.when(pl.program_id(0) == 0)
    def _():
        first = first_ref[0]
        pos = lax.broadcasted_iota(jnp.int32, (8, rows), 1)
        q_block = ((pos % per_owner) * owners + pos // per_owner) // BLOCK
        dead = jnp.full((8, rows), jnp.inf, jnp.float32)
        biases = [jnp.full((8, rows), masked_fill, jnp.float32) for _ in range(k_blocks)]
        for a in range(q_blocks):
            for b in range(k_blocks):
                hit = jnp.int32(0)
                for slot in range(max_sel):
                    found = (list_ref[a, slot] == first + b) & (slot < count_ref[a])
                    hit = jnp.maximum(hit, jnp.where(found, 1, 0).astype(jnp.int32))
                live = (q_block == a) & (hit > 0)
                biases[b] = jnp.where(live, 0.0, biases[b])
                dead = jnp.where(live, 0.0, dead)
        for b in range(k_blocks):
            bias_ref[b * BLOCK : (b + 1) * BLOCK, :] = jnp.broadcast_to(biases[b][0:1, :], (BLOCK, rows))
        dead_ref[...] = dead

    score_scale = 1.0 / HEAD_DIM**0.5
    dead_row = dead_ref[0:1, :]
    for hl in range(head_share):
        cols = slice(hl * HEAD_DIM, (hl + 1) * HEAD_DIM)
        q_scr[...] = q_ref[:, cols].astype(jnp.float32)
        q_perm = jnp.concatenate(
            [q_scr[pl.ds(r, per_owner, stride=owners), :] for r in range(owners)], axis=0
        ).astype(jnp.bfloat16)
        scores = lax.dot_general(
            k_ref[:, cols], q_perm, (((1,), (1,)), ((), ())), preferred_element_type=jnp.float32
        )
        scores = scores * score_scale + bias_ref[...]
        seg_max = jnp.max(scores, axis=0, keepdims=True)
        probs = jnp.exp(scores - (seg_max + dead_row))
        seg_total = jnp.sum(probs, axis=0, keepdims=True)
        seg_out = lax.dot_general(
            probs.astype(jnp.bfloat16), v_ref[:, cols], (((0,), (0,)), ((), ())),
            preferred_element_type=jnp.float32,
        )
        part_ref[:, hl] = seg_out.reshape(owners, per_owner, HEAD_DIM).astype(jnp.bfloat16)
        stat_ref[0, hl : hl + 1, :] = seg_max
        stat_ref[1, hl : hl + 1, :] = seg_total


def local_attention(queries, keys, values, block_list, block_count, first_block, owners, shards):
    rows = queries.shape[0]
    per_owner = rows // owners
    ctx_span = keys.shape[0]
    step_heads = HEADS_PER_STEP
    step_width = step_heads * HEAD_DIM
    q_blocks = rows // BLOCK
    k_blocks = ctx_span // BLOCK
    max_sel = block_list.shape[1]
    shape = (rows, owners, per_owner, step_heads, q_blocks, k_blocks, max_sel)
    grid_spec = pltpu.PrefetchScalarGridSpec(
        num_scalar_prefetch=3,
        grid=(HEADS // step_heads,),
        in_specs=[
            pl.BlockSpec((rows, step_width), lambda g, *_: (0, g)),
            pl.BlockSpec((ctx_span, step_width), lambda g, *_: (0, g)),
            pl.BlockSpec((ctx_span, step_width), lambda g, *_: (0, g)),
        ],
        out_specs=[
            pl.BlockSpec((owners, step_heads, per_owner, HEAD_DIM), lambda g, *_: (0, g, 0, 0)),
            pl.BlockSpec((2, step_heads, rows), lambda g, *_: (0, g, 0)),
        ],
        scratch_shapes=[
            pltpu.VMEM((ctx_span, rows), jnp.float32),
            pltpu.VMEM((8, rows), jnp.float32),
            pltpu.VMEM((rows, HEAD_DIM), jnp.float32),
        ],
    )
    flops = 4 * HEADS * rows * ctx_span * HEAD_DIM
    return pl.pallas_call(
        functools.partial(attention_kernel, shape),
        grid_spec=grid_spec,
        out_shape=[
            jax.ShapeDtypeStruct((owners, HEADS, per_owner, HEAD_DIM), jnp.bfloat16),
            jax.ShapeDtypeStruct((2, HEADS, rows), jnp.float32),
        ],
        compiler_params=pltpu.CompilerParams(dimension_semantics=("arbitrary",)),
        cost_estimate=pl.CostEstimate(
            flops=flops,
            transcendentals=HEADS * rows * ctx_span,
            bytes_accessed=2 * (queries.size + keys.size + values.size) + 2 * rows * HEADS * HEAD_DIM,
        ),
    )(block_list, block_count, first_block, queries, keys, values)


def split_three(x):
    hi = lax.reduce_precision(x, exponent_bits=8, mantissa_bits=7)
    rest = x - hi
    mid = lax.reduce_precision(rest, exponent_bits=8, mantissa_bits=7)
    lo = lax.reduce_precision(rest - mid, exponent_bits=8, mantissa_bits=7)
    return jnp.stack([hi, mid, lo], axis=1).astype(jnp.bfloat16)


def join_three(parts):
    parts = parts.astype(jnp.float32)
    return (parts[:, 0] + parts[:, 1]) + parts[:, 2]


def local(queries, keys, values, block_list, block_count):
    row_count = queries.shape[0]
    ctx_span = keys.shape[0]
    shards = lax.axis_size("ctx")
    owners = lax.axis_size("row")
    per_owner = row_count // owners
    head_share = HEADS // shards
    share_width = head_share * HEAD_DIM
    blocks_here = ctx_span // BLOCK
    first_block = (lax.axis_index("ctx") * blocks_here).astype(jnp.int32).reshape(1)
    part, stat = local_attention(
        queries, keys, values, block_list.astype(jnp.int32), block_count.astype(jnp.int32), first_block, owners, shards
    )
    part_low = part.reshape(owners * shards, head_share * per_owner, HEAD_DIM)
    stats = jnp.transpose(stat.reshape(2, shards, head_share, owners, per_owner), (3, 1, 0, 2, 4))
    stats = stats.reshape(owners * shards, 2, head_share, per_owner)
    stat_count = 3 * 2 * head_share * per_owner
    stat_rows = -(-stat_count // HEAD_DIM)
    stat_low = split_three(stats).reshape(owners * shards, stat_count)
    stat_low = jnp.pad(stat_low, ((0, 0), (0, stat_rows * HEAD_DIM - stat_count)))
    payload = jnp.concatenate(
        [part_low, stat_low.reshape(owners * shards, stat_rows, HEAD_DIM)], axis=1
    )
    arrived = lax.all_to_all(payload, ("row", "ctx"), 0, 0, tiled=True)
    arrived = arrived.reshape(owners, shards, head_share * per_owner + stat_rows, HEAD_DIM)
    part_in = arrived[:, :, : head_share * per_owner].reshape(owners, shards, head_share, per_owner, HEAD_DIM)
    stat_in = arrived[:, :, head_share * per_owner :].reshape(owners * shards, stat_rows * HEAD_DIM)
    stats_in = join_three(
        stat_in[:, :stat_count].reshape(owners * shards, 3, 2, head_share, per_owner)
    ).reshape(owners, shards, 2, head_share, per_owner)
    maxima = stats_in[:, :, 0]
    totals = stats_in[:, :, 1]
    row_best = jnp.max(maxima, axis=1)
    weight = jnp.exp(maxima - row_best[:, None])
    total_sum = jnp.sum(totals * weight, axis=1)
    numerator = jnp.sum(part_in.astype(jnp.float32) * weight[..., None], axis=1)
    attended = numerator / total_sum[..., None]
    attended_low = jnp.transpose(attended, (0, 2, 1, 3)).reshape(row_count, share_width)
    return attended_low.astype(jnp.bfloat16)


def solution(mesh):
    return jax.shard_map(
        local,
        mesh=mesh,
        in_specs=(P("row", None), P("ctx", None), P("ctx", None), P("row", None), P("row")),
        out_specs=P("row", "ctx"),
        check_vma=False,
    )
```

```python
import functools

import jax
import jax.numpy as jnp
from jax import lax
from jax.experimental import pallas as pl
from jax.experimental.pallas import tpu as pltpu
from jax.experimental.layout import Layout, with_layout_constraint
from jax.sharding import PartitionSpec as P

HEADS = 16
HEAD_DIM = 128
BLOCK = 128
HEADS_PER_STEP = 16


masked_fill = -1e30


def attention_kernel(shape, list_ref, count_ref, first_ref, q_ref, k_ref, v_ref, part_ref, stat_ref,
                     bias_ref, dead_ref, q_scr):
    rows, owners, per_owner, head_share, q_blocks, k_blocks, max_sel = shape

    @pl.when(pl.program_id(0) == 0)
    def _():
        first = first_ref[0]
        pos = lax.broadcasted_iota(jnp.int32, (8, rows), 1)
        q_block = ((pos % per_owner) * owners + pos // per_owner) // BLOCK
        dead = jnp.full((8, rows), jnp.inf, jnp.float32)
        biases = [jnp.full((8, rows), masked_fill, jnp.float32) for _ in range(k_blocks)]
        for a in range(q_blocks):
            for b in range(k_blocks):
                hit = jnp.int32(0)
                for slot in range(max_sel):
                    found = (list_ref[a, slot] == first + b) & (slot < count_ref[a])
                    hit = jnp.maximum(hit, jnp.where(found, 1, 0).astype(jnp.int32))
                live = (q_block == a) & (hit > 0)
                biases[b] = jnp.where(live, 0.0, biases[b])
                dead = jnp.where(live, 0.0, dead)
        for b in range(k_blocks):
            bias_ref[b * BLOCK : (b + 1) * BLOCK, :] = jnp.broadcast_to(biases[b][0:1, :], (BLOCK, rows))
        dead_ref[...] = dead

    score_scale = 1.0 / HEAD_DIM**0.5
    dead_row = dead_ref[0:1, :]
    for hl in range(head_share):
        cols = slice(hl * HEAD_DIM, (hl + 1) * HEAD_DIM)
        q_scr[...] = q_ref[:, cols].astype(jnp.float32)
        q_perm = jnp.concatenate(
            [q_scr[pl.ds(r, per_owner, stride=owners), :] for r in range(owners)], axis=0
        ).astype(jnp.bfloat16)
        scores = lax.dot_general(
            k_ref[:, cols], q_perm, (((1,), (1,)), ((), ())), preferred_element_type=jnp.float32
        )
        scores = scores * score_scale + bias_ref[...]
        seg_max = jnp.max(scores, axis=0, keepdims=True)
        probs = jnp.exp(scores - (seg_max + dead_row))
        seg_total = jnp.sum(probs, axis=0, keepdims=True)
        seg_out = lax.dot_general(
            probs.astype(jnp.bfloat16), v_ref[:, cols], (((0,), (0,)), ((), ())),
            preferred_element_type=jnp.float32,
        )
        part_ref[:, hl] = seg_out.reshape(owners, per_owner, HEAD_DIM).astype(jnp.bfloat16)
        stat_ref[0, hl : hl + 1, :] = seg_max
        stat_ref[1, hl : hl + 1, :] = seg_total


def local_attention(queries, keys, values, block_list, block_count, first_block, owners, shards):
    rows = queries.shape[0]
    per_owner = rows // owners
    ctx_span = keys.shape[0]
    step_heads = HEADS_PER_STEP
    step_width = step_heads * HEAD_DIM
    q_blocks = rows // BLOCK
    k_blocks = ctx_span // BLOCK
    max_sel = block_list.shape[1]
    shape = (rows, owners, per_owner, step_heads, q_blocks, k_blocks, max_sel)
    grid_spec = pltpu.PrefetchScalarGridSpec(
        num_scalar_prefetch=3,
        grid=(HEADS // step_heads,),
        in_specs=[
            pl.BlockSpec((rows, step_width), lambda g, *_: (0, g)),
            pl.BlockSpec((ctx_span, step_width), lambda g, *_: (0, g)),
            pl.BlockSpec((ctx_span, step_width), lambda g, *_: (0, g)),
        ],
        out_specs=[
            pl.BlockSpec((owners, step_heads, per_owner, HEAD_DIM), lambda g, *_: (0, g, 0, 0)),
            pl.BlockSpec((2, step_heads, rows), lambda g, *_: (0, g, 0)),
        ],
        scratch_shapes=[
            pltpu.VMEM((ctx_span, rows), jnp.float32),
            pltpu.VMEM((8, rows), jnp.float32),
            pltpu.VMEM((rows, HEAD_DIM), jnp.float32),
        ],
    )
    flops = 4 * HEADS * rows * ctx_span * HEAD_DIM
    return pl.pallas_call(
        functools.partial(attention_kernel, shape),
        grid_spec=grid_spec,
        out_shape=[
            jax.ShapeDtypeStruct((owners, HEADS, per_owner, HEAD_DIM), jnp.bfloat16),
            jax.ShapeDtypeStruct((2, HEADS, rows), jnp.float32),
        ],
        compiler_params=pltpu.CompilerParams(dimension_semantics=("arbitrary",)),
        cost_estimate=pl.CostEstimate(
            flops=flops,
            transcendentals=HEADS * rows * ctx_span,
            bytes_accessed=2 * (queries.size + keys.size + values.size) + 2 * rows * HEADS * HEAD_DIM,
        ),
    )(block_list, block_count, first_block, queries, keys, values)


def split_three(x):
    hi = lax.reduce_precision(x, exponent_bits=8, mantissa_bits=7)
    rest = x - hi
    mid = lax.reduce_precision(rest, exponent_bits=8, mantissa_bits=7)
    lo = lax.reduce_precision(rest - mid, exponent_bits=8, mantissa_bits=7)
    return jnp.stack([hi, mid, lo], axis=1).astype(jnp.bfloat16)


def join_three(parts):
    parts = parts.astype(jnp.float32)
    return (parts[:, 0] + parts[:, 1]) + parts[:, 2]


def local(queries, keys, values, block_list, block_count):
    row_count = queries.shape[0]
    ctx_span = keys.shape[0]
    shards = lax.axis_size("ctx")
    owners = lax.axis_size("row")
    per_owner = row_count // owners
    head_share = HEADS // shards
    share_width = head_share * HEAD_DIM
    blocks_here = ctx_span // BLOCK
    first_block = (lax.axis_index("ctx") * blocks_here).astype(jnp.int32).reshape(1)
    part, stat = local_attention(
        queries, keys, values, block_list.astype(jnp.int32), block_count.astype(jnp.int32), first_block, owners, shards
    )
    part_low = part.reshape(owners * shards, head_share * per_owner, HEAD_DIM)
    stats = jnp.transpose(stat.reshape(2, shards, head_share, owners, per_owner), (3, 1, 0, 2, 4))
    stats = stats.reshape(owners * shards, 2, head_share, per_owner)
    stat_count = 3 * 2 * head_share * per_owner
    stat_rows = -(-stat_count // HEAD_DIM)
    stat_low = split_three(stats).reshape(owners * shards, stat_count)
    stat_low = jnp.pad(stat_low, ((0, 0), (0, stat_rows * HEAD_DIM - stat_count)))
    payload = jnp.concatenate(
        [part_low, stat_low.reshape(owners * shards, stat_rows, HEAD_DIM)], axis=1
    )
    arrived = lax.all_to_all(payload, ("row", "ctx"), 0, 0, tiled=True)
    arrived = with_layout_constraint(arrived, Layout(major_to_minor=(0, 1, 2)))
    arrived = arrived.reshape(owners, shards, head_share * per_owner + stat_rows, HEAD_DIM)
    part_in = arrived[:, :, : head_share * per_owner].reshape(owners, shards, head_share, per_owner, HEAD_DIM)
    stat_in = arrived[:, :, head_share * per_owner :].reshape(owners * shards, stat_rows * HEAD_DIM)
    stats_in = join_three(
        stat_in[:, :stat_count].reshape(owners * shards, 3, 2, head_share, per_owner)
    ).reshape(owners, shards, 2, head_share, per_owner)
    maxima = stats_in[:, :, 0]
    totals = stats_in[:, :, 1]
    row_best = jnp.max(maxima, axis=1)
    weight = jnp.exp(maxima - row_best[:, None])
    total_sum = jnp.sum(totals * weight, axis=1)
    numerator = jnp.sum(part_in.astype(jnp.float32) * weight[..., None], axis=1)
    attended = numerator / total_sum[..., None]
    attended_low = jnp.transpose(attended, (0, 2, 1, 3)).reshape(row_count, share_width)
    return attended_low.astype(jnp.bfloat16)


def solution(mesh):
    return jax.shard_map(
        local,
        mesh=mesh,
        in_specs=(P("row", None), P("ctx", None), P("ctx", None), P("row", None), P("row")),
        out_specs=P("row", "ctx"),
        check_vma=False,
    )
```

```python
import functools

import jax
import jax.numpy as jnp
from jax import lax
from jax.experimental import pallas as pl
from jax.experimental.pallas import tpu as pltpu
from jax.experimental.layout import Layout, with_layout_constraint
from jax.sharding import PartitionSpec as P

HEADS = 16
HEAD_DIM = 128
BLOCK = 128
HEADS_PER_STEP = 8


masked_fill = -1e30


def attention_kernel(shape, list_ref, count_ref, first_ref, q_ref, k_ref, v_ref, part_ref, stat_ref,
                     bias_ref, dead_ref, q_scr):
    rows, owners, per_owner, head_share, q_blocks, k_blocks, max_sel = shape

    @pl.when(pl.program_id(0) == 0)
    def _():
        first = first_ref[0]
        pos = lax.broadcasted_iota(jnp.int32, (8, rows), 1)
        q_block = ((pos % per_owner) * owners + pos // per_owner) // BLOCK
        dead = jnp.full((8, rows), jnp.inf, jnp.float32)
        biases = [jnp.full((8, rows), masked_fill, jnp.float32) for _ in range(k_blocks)]
        for a in range(q_blocks):
            for b in range(k_blocks):
                hit = jnp.int32(0)
                for slot in range(max_sel):
                    found = (list_ref[a, slot] == first + b) & (slot < count_ref[a])
                    hit = jnp.maximum(hit, jnp.where(found, 1, 0).astype(jnp.int32))
                live = (q_block == a) & (hit > 0)
                biases[b] = jnp.where(live, 0.0, biases[b])
                dead = jnp.where(live, 0.0, dead)
        for b in range(k_blocks):
            bias_ref[b * BLOCK : (b + 1) * BLOCK, :] = jnp.broadcast_to(biases[b][0:1, :], (BLOCK, rows))
        dead_ref[...] = dead

    score_scale = 1.0 / HEAD_DIM**0.5
    dead_row = dead_ref[0:1, :]
    for hl in range(head_share):
        cols = slice(hl * HEAD_DIM, (hl + 1) * HEAD_DIM)
        q_scr[...] = q_ref[:, cols].astype(jnp.float32)
        q_perm = jnp.concatenate(
            [q_scr[pl.ds(r, per_owner, stride=owners), :] for r in range(owners)], axis=0
        ).astype(jnp.bfloat16)
        scores = lax.dot_general(
            k_ref[:, cols], q_perm, (((1,), (1,)), ((), ())), preferred_element_type=jnp.float32
        )
        scores = scores * score_scale + bias_ref[...]
        seg_max = jnp.max(scores, axis=0, keepdims=True)
        probs = jnp.exp(scores - (seg_max + dead_row))
        seg_total = jnp.sum(probs, axis=0, keepdims=True)
        seg_out = lax.dot_general(
            probs.astype(jnp.bfloat16), v_ref[:, cols], (((0,), (0,)), ((), ())),
            preferred_element_type=jnp.float32,
        )
        part_ref[:, hl] = seg_out.reshape(owners, per_owner, HEAD_DIM).astype(jnp.bfloat16)
        stat_ref[0, hl : hl + 1, :] = seg_max
        stat_ref[1, hl : hl + 1, :] = seg_total


def local_attention(queries, keys, values, block_list, block_count, first_block, owners, shards):
    rows = queries.shape[0]
    per_owner = rows // owners
    ctx_span = keys.shape[0]
    step_heads = HEADS_PER_STEP
    step_width = step_heads * HEAD_DIM
    q_blocks = rows // BLOCK
    k_blocks = ctx_span // BLOCK
    max_sel = block_list.shape[1]
    shape = (rows, owners, per_owner, step_heads, q_blocks, k_blocks, max_sel)
    grid_spec = pltpu.PrefetchScalarGridSpec(
        num_scalar_prefetch=3,
        grid=(HEADS // step_heads,),
        in_specs=[
            pl.BlockSpec((rows, step_width), lambda g, *_: (0, g)),
            pl.BlockSpec((ctx_span, step_width), lambda g, *_: (0, g)),
            pl.BlockSpec((ctx_span, step_width), lambda g, *_: (0, g)),
        ],
        out_specs=[
            pl.BlockSpec((owners, step_heads, per_owner, HEAD_DIM), lambda g, *_: (0, g, 0, 0)),
            pl.BlockSpec((2, step_heads, rows), lambda g, *_: (0, g, 0)),
        ],
        scratch_shapes=[
            pltpu.VMEM((ctx_span, rows), jnp.float32),
            pltpu.VMEM((8, rows), jnp.float32),
            pltpu.VMEM((rows, HEAD_DIM), jnp.float32),
        ],
    )
    flops = 4 * HEADS * rows * ctx_span * HEAD_DIM
    return pl.pallas_call(
        functools.partial(attention_kernel, shape),
        grid_spec=grid_spec,
        out_shape=[
            jax.ShapeDtypeStruct((owners, HEADS, per_owner, HEAD_DIM), jnp.bfloat16),
            jax.ShapeDtypeStruct((2, HEADS, rows), jnp.float32),
        ],
        compiler_params=pltpu.CompilerParams(dimension_semantics=("arbitrary",)),
        cost_estimate=pl.CostEstimate(
            flops=flops,
            transcendentals=HEADS * rows * ctx_span,
            bytes_accessed=2 * (queries.size + keys.size + values.size) + 2 * rows * HEADS * HEAD_DIM,
        ),
    )(block_list, block_count, first_block, queries, keys, values)


def split_three(x):
    hi = lax.reduce_precision(x, exponent_bits=8, mantissa_bits=7)
    rest = x - hi
    mid = lax.reduce_precision(rest, exponent_bits=8, mantissa_bits=7)
    lo = lax.reduce_precision(rest - mid, exponent_bits=8, mantissa_bits=7)
    return jnp.stack([hi, mid, lo], axis=1).astype(jnp.bfloat16)


def join_three(parts):
    parts = parts.astype(jnp.float32)
    return (parts[:, 0] + parts[:, 1]) + parts[:, 2]


def local(queries, keys, values, block_list, block_count):
    row_count = queries.shape[0]
    ctx_span = keys.shape[0]
    shards = lax.axis_size("ctx")
    owners = lax.axis_size("row")
    per_owner = row_count // owners
    head_share = HEADS // shards
    share_width = head_share * HEAD_DIM
    blocks_here = ctx_span // BLOCK
    first_block = (lax.axis_index("ctx") * blocks_here).astype(jnp.int32).reshape(1)
    part, stat = local_attention(
        queries, keys, values, block_list.astype(jnp.int32), block_count.astype(jnp.int32), first_block, owners, shards
    )
    part_low = part.reshape(owners * shards, head_share * per_owner, HEAD_DIM)
    stats = jnp.transpose(stat.reshape(2, shards, head_share, owners, per_owner), (3, 1, 0, 2, 4))
    stats = stats.reshape(owners * shards, 2, head_share, per_owner)
    stat_count = 3 * 2 * head_share * per_owner
    stat_rows = -(-stat_count // HEAD_DIM)
    stat_low = split_three(stats).reshape(owners * shards, stat_count)
    stat_low = jnp.pad(stat_low, ((0, 0), (0, stat_rows * HEAD_DIM - stat_count)))
    payload = jnp.concatenate(
        [part_low, stat_low.reshape(owners * shards, stat_rows, HEAD_DIM)], axis=1
    )
    arrived = lax.all_to_all(payload, ("row", "ctx"), 0, 0, tiled=True)
    arrived = with_layout_constraint(arrived, Layout(major_to_minor=(0, 1, 2)))
    arrived = arrived.reshape(owners, shards, head_share * per_owner + stat_rows, HEAD_DIM)
    part_in = arrived[:, :, : head_share * per_owner].reshape(owners, shards, head_share, per_owner, HEAD_DIM)
    stat_in = arrived[:, :, head_share * per_owner :].reshape(owners * shards, stat_rows * HEAD_DIM)
    stats_in = join_three(
        stat_in[:, :stat_count].reshape(owners * shards, 3, 2, head_share, per_owner)
    ).reshape(owners, shards, 2, head_share, per_owner)
    maxima = stats_in[:, :, 0]
    totals = stats_in[:, :, 1]
    row_best = jnp.max(maxima, axis=1)
    weight = jnp.exp(maxima - row_best[:, None])
    total_sum = jnp.sum(totals * weight, axis=1)
    numerator = jnp.sum(part_in.astype(jnp.float32) * weight[..., None], axis=1)
    attended = numerator / total_sum[..., None]
    attended_low = jnp.transpose(attended, (0, 2, 1, 3)).reshape(row_count, share_width)
    return attended_low.astype(jnp.bfloat16)


def solution(mesh):
    return jax.shard_map(
        local,
        mesh=mesh,
        in_specs=(P("row", None), P("ctx", None), P("ctx", None), P("row", None), P("row")),
        out_specs=P("row", "ctx"),
        check_vma=False,
    )
```

```python
import functools

import jax
import jax.numpy as jnp
from jax import lax
from jax.experimental import pallas as pl
from jax.experimental.pallas import tpu as pltpu
from jax.experimental.layout import Layout, with_layout_constraint
from jax.sharding import PartitionSpec as P

HEADS = 16
HEAD_DIM = 128
BLOCK = 128
HEADS_PER_STEP = 16


masked_fill = -1e30


def attention_kernel(shape, list_ref, count_ref, first_ref, q_ref, k_ref, v_ref, part_ref, stat_ref,
                     bias_ref, dead_ref, q_scr):
    rows, owners, per_owner, head_share, q_blocks, k_blocks, max_sel = shape

    @pl.when(pl.program_id(0) == 0)
    def _():
        first = first_ref[0]
        pos = lax.broadcasted_iota(jnp.int32, (8, rows), 1)
        q_block = ((pos % per_owner) * owners + pos // per_owner) // BLOCK
        dead = jnp.full((8, rows), jnp.inf, jnp.float32)
        biases = [jnp.full((8, rows), masked_fill, jnp.float32) for _ in range(k_blocks)]
        for a in range(q_blocks):
            for b in range(k_blocks):
                hit = jnp.int32(0)
                for slot in range(max_sel):
                    found = (list_ref[a, slot] == first + b) & (slot < count_ref[a])
                    hit = jnp.maximum(hit, jnp.where(found, 1, 0).astype(jnp.int32))
                live = (q_block == a) & (hit > 0)
                biases[b] = jnp.where(live, 0.0, biases[b])
                dead = jnp.where(live, 0.0, dead)
        for b in range(k_blocks):
            bias_ref[b * BLOCK : (b + 1) * BLOCK, :] = jnp.broadcast_to(biases[b][0:1, :], (BLOCK, rows))
        dead_ref[...] = dead

    score_scale = 1.0 / HEAD_DIM**0.5
    dead_row = dead_ref[0:1, :]
    for hl in range(head_share):
        cols = slice(hl * HEAD_DIM, (hl + 1) * HEAD_DIM)
        q_scr[...] = q_ref[:, cols].astype(jnp.float32)
        q_perm = jnp.concatenate(
            [q_scr[pl.ds(r, per_owner, stride=owners), :] for r in range(owners)], axis=0
        ).astype(jnp.bfloat16)
        scores = lax.dot_general(
            k_ref[:, cols], q_perm, (((1,), (1,)), ((), ())), preferred_element_type=jnp.float32
        )
        scores = scores * score_scale + bias_ref[...]
        seg_max = jnp.max(scores, axis=0, keepdims=True)
        probs = jnp.exp(scores - (seg_max + dead_row))
        seg_total = jnp.sum(probs, axis=0, keepdims=True)
        seg_out = lax.dot_general(
            probs.astype(jnp.bfloat16), v_ref[:, cols], (((0,), (0,)), ((), ())),
            preferred_element_type=jnp.float32,
        )
        part_ref[:, hl] = seg_out.reshape(owners, per_owner, HEAD_DIM).astype(jnp.bfloat16)
        stat_ref[0, hl : hl + 1, :] = seg_max
        stat_ref[1, hl : hl + 1, :] = seg_total


def local_attention(queries, keys, values, block_list, block_count, first_block, owners, shards):
    rows = queries.shape[0]
    per_owner = rows // owners
    ctx_span = keys.shape[0]
    step_heads = HEADS_PER_STEP
    step_width = step_heads * HEAD_DIM
    q_blocks = rows // BLOCK
    k_blocks = ctx_span // BLOCK
    max_sel = block_list.shape[1]
    shape = (rows, owners, per_owner, step_heads, q_blocks, k_blocks, max_sel)
    grid_spec = pltpu.PrefetchScalarGridSpec(
        num_scalar_prefetch=3,
        grid=(HEADS // step_heads,),
        in_specs=[
            pl.BlockSpec((rows, step_width), lambda g, *_: (0, g)),
            pl.BlockSpec((ctx_span, step_width), lambda g, *_: (0, g)),
            pl.BlockSpec((ctx_span, step_width), lambda g, *_: (0, g)),
        ],
        out_specs=[
            pl.BlockSpec((owners, step_heads, per_owner, HEAD_DIM), lambda g, *_: (0, g, 0, 0)),
            pl.BlockSpec((2, step_heads, rows), lambda g, *_: (0, g, 0)),
        ],
        scratch_shapes=[
            pltpu.VMEM((ctx_span, rows), jnp.float32),
            pltpu.VMEM((8, rows), jnp.float32),
            pltpu.VMEM((rows, HEAD_DIM), jnp.float32),
        ],
    )
    flops = 4 * HEADS * rows * ctx_span * HEAD_DIM
    return pl.pallas_call(
        functools.partial(attention_kernel, shape),
        grid_spec=grid_spec,
        out_shape=[
            jax.ShapeDtypeStruct((owners, HEADS, per_owner, HEAD_DIM), jnp.bfloat16),
            jax.ShapeDtypeStruct((2, HEADS, rows), jnp.float32),
        ],
        compiler_params=pltpu.CompilerParams(dimension_semantics=("arbitrary",)),
        cost_estimate=pl.CostEstimate(
            flops=flops,
            transcendentals=HEADS * rows * ctx_span,
            bytes_accessed=2 * (queries.size + keys.size + values.size) + 2 * rows * HEADS * HEAD_DIM,
        ),
    )(block_list, block_count, first_block, queries, keys, values)


def split_three(x):
    hi = lax.reduce_precision(x, exponent_bits=8, mantissa_bits=7)
    rest = x - hi
    mid = lax.reduce_precision(rest, exponent_bits=8, mantissa_bits=7)
    lo = lax.reduce_precision(rest - mid, exponent_bits=8, mantissa_bits=7)
    return jnp.stack([hi, mid, lo], axis=1).astype(jnp.bfloat16)


def join_three(parts):
    parts = parts.astype(jnp.float32)
    return (parts[:, 0] + parts[:, 1]) + parts[:, 2]


def local(queries, keys, values, block_list, block_count):
    row_count = queries.shape[0]
    ctx_span = keys.shape[0]
    shards = lax.axis_size("ctx")
    owners = lax.axis_size("row")
    per_owner = row_count // owners
    head_share = HEADS // shards
    share_width = head_share * HEAD_DIM
    blocks_here = ctx_span // BLOCK
    first_block = (lax.axis_index("ctx") * blocks_here).astype(jnp.int32).reshape(1)
    part, stat = local_attention(
        queries, keys, values, block_list.astype(jnp.int32), block_count.astype(jnp.int32), first_block, owners, shards
    )
    part_low = part.reshape(owners * shards, head_share * per_owner, HEAD_DIM)
    stats = jnp.transpose(stat.reshape(2, shards, head_share, owners, per_owner), (3, 1, 0, 2, 4))
    stats = stats.reshape(owners * shards, 2, head_share, per_owner)
    stat_count = 3 * 2 * head_share * per_owner
    stat_rows = -(-stat_count // HEAD_DIM)
    stat_low = split_three(stats).reshape(owners * shards, stat_count)
    stat_low = jnp.pad(stat_low, ((0, 0), (0, stat_rows * HEAD_DIM - stat_count)))
    payload = jnp.concatenate(
        [part_low, stat_low.reshape(owners * shards, stat_rows, HEAD_DIM)], axis=1
    )
    arrived = lax.all_to_all(payload, ("row", "ctx"), 0, 0, tiled=True)
    arrived = with_layout_constraint(arrived, Layout(major_to_minor=(0, 1, 2)))
    arrived = arrived.reshape(owners, shards, head_share * per_owner + stat_rows, HEAD_DIM)
    part_in = arrived[:, :, : head_share * per_owner].reshape(owners, shards, head_share, per_owner, HEAD_DIM)
    stat_in = arrived[:, :, head_share * per_owner :].reshape(owners * shards, stat_rows * HEAD_DIM)
    stats_in = join_three(
        stat_in[:, :stat_count].reshape(owners * shards, 3, 2, head_share, per_owner)
    ).reshape(owners, shards, 2, head_share, per_owner)
    maxima = stats_in[:, :, 0]
    totals = stats_in[:, :, 1]
    row_best = jnp.max(maxima, axis=1)
    weight = jnp.exp(maxima - row_best[:, None])
    total_sum = jnp.sum(totals * weight, axis=1)
    numerator = jnp.sum(part_in.astype(jnp.float32) * weight[..., None], axis=1)
    attended = numerator / total_sum[..., None]
    attended_low = jnp.transpose(attended, (0, 2, 1, 3)).astype(jnp.bfloat16)
    attended_low = with_layout_constraint(attended_low, Layout(major_to_minor=(0, 1, 2, 3)))
    return attended_low.reshape(row_count, share_width)


def solution(mesh):
    return jax.shard_map(
        local,
        mesh=mesh,
        in_specs=(P("row", None), P("ctx", None), P("ctx", None), P("row", None), P("row")),
        out_specs=P("row", "ctx"),
        check_vma=False,
    )
```

```python
import functools

import jax
import jax.numpy as jnp
from jax import lax
from jax.experimental import pallas as pl
from jax.experimental.pallas import tpu as pltpu
from jax.experimental.layout import Layout, with_layout_constraint
from jax.sharding import PartitionSpec as P

HEADS = 16
HEAD_DIM = 128
BLOCK = 128
HEADS_PER_STEP = 16


masked_fill = -1e30


def attention_kernel(shape, list_ref, count_ref, first_ref, q_ref, k_ref, v_ref, part_ref, stat_ref,
                     bias_ref, dead_ref, q_scr):
    rows, owners, per_owner, head_share, q_blocks, k_blocks, max_sel = shape

    @pl.when(pl.program_id(0) == 0)
    def _():
        first = first_ref[0]
        pos = lax.broadcasted_iota(jnp.int32, (8, rows), 1)
        q_block = ((pos % per_owner) * owners + pos // per_owner) // BLOCK
        dead = jnp.full((8, rows), jnp.inf, jnp.float32)
        biases = [jnp.full((8, rows), masked_fill, jnp.float32) for _ in range(k_blocks)]
        for a in range(q_blocks):
            for b in range(k_blocks):
                hit = jnp.int32(0)
                for slot in range(max_sel):
                    found = (list_ref[a, slot] == first + b) & (slot < count_ref[a])
                    hit = jnp.maximum(hit, jnp.where(found, 1, 0).astype(jnp.int32))
                live = (q_block == a) & (hit > 0)
                biases[b] = jnp.where(live, 0.0, biases[b])
                dead = jnp.where(live, 0.0, dead)
        for b in range(k_blocks):
            bias_ref[b * BLOCK : (b + 1) * BLOCK, :] = jnp.broadcast_to(biases[b][0:1, :], (BLOCK, rows))
        dead_ref[...] = dead

    score_scale = 1.0 / HEAD_DIM**0.5
    dead_row = dead_ref[0:1, :]
    for hl in range(head_share):
        cols = slice(hl * HEAD_DIM, (hl + 1) * HEAD_DIM)
        q_scr[...] = q_ref[:, cols].astype(jnp.float32)
        q_perm = jnp.concatenate(
            [q_scr[pl.ds(r, per_owner, stride=owners), :] for r in range(owners)], axis=0
        ).astype(jnp.bfloat16)
        scores = lax.dot_general(
            k_ref[:, cols], q_perm, (((1,), (1,)), ((), ())), preferred_element_type=jnp.float32
        )
        scores = scores * score_scale + bias_ref[...]
        seg_max = jnp.max(scores, axis=0, keepdims=True)
        probs = jnp.exp(scores - (seg_max + dead_row))
        seg_total = jnp.sum(probs, axis=0, keepdims=True)
        seg_out = lax.dot_general(
            probs.astype(jnp.bfloat16), v_ref[:, cols], (((0,), (0,)), ((), ())),
            preferred_element_type=jnp.float32,
        )
        part_ref[:, hl] = seg_out.reshape(owners, per_owner, HEAD_DIM).astype(jnp.bfloat16)
        stat_ref[0, hl : hl + 1, :] = seg_max
        stat_ref[1, hl : hl + 1, :] = seg_total


def local_attention(queries, keys, values, block_list, block_count, first_block, owners, shards):
    rows = queries.shape[0]
    per_owner = rows // owners
    ctx_span = keys.shape[0]
    step_heads = HEADS_PER_STEP
    step_width = step_heads * HEAD_DIM
    q_blocks = rows // BLOCK
    k_blocks = ctx_span // BLOCK
    max_sel = block_list.shape[1]
    shape = (rows, owners, per_owner, step_heads, q_blocks, k_blocks, max_sel)
    grid_spec = pltpu.PrefetchScalarGridSpec(
        num_scalar_prefetch=3,
        grid=(HEADS // step_heads,),
        in_specs=[
            pl.BlockSpec((rows, step_width), lambda g, *_: (0, g)),
            pl.BlockSpec((ctx_span, step_width), lambda g, *_: (0, g)),
            pl.BlockSpec((ctx_span, step_width), lambda g, *_: (0, g)),
        ],
        out_specs=[
            pl.BlockSpec((owners, step_heads, per_owner, HEAD_DIM), lambda g, *_: (0, g, 0, 0)),
            pl.BlockSpec((2, step_heads, rows), lambda g, *_: (0, g, 0)),
        ],
        scratch_shapes=[
            pltpu.VMEM((ctx_span, rows), jnp.float32),
            pltpu.VMEM((8, rows), jnp.float32),
            pltpu.VMEM((rows, HEAD_DIM), jnp.float32),
        ],
    )
    flops = 4 * HEADS * rows * ctx_span * HEAD_DIM
    return pl.pallas_call(
        functools.partial(attention_kernel, shape),
        grid_spec=grid_spec,
        out_shape=[
            jax.ShapeDtypeStruct((owners, HEADS, per_owner, HEAD_DIM), jnp.bfloat16),
            jax.ShapeDtypeStruct((2, HEADS, rows), jnp.float32),
        ],
        compiler_params=pltpu.CompilerParams(dimension_semantics=("arbitrary",)),
        cost_estimate=pl.CostEstimate(
            flops=flops,
            transcendentals=HEADS * rows * ctx_span,
            bytes_accessed=2 * (queries.size + keys.size + values.size) + 2 * rows * HEADS * HEAD_DIM,
        ),
    )(block_list, block_count, first_block, queries, keys, values)


def split_three(x):
    hi = lax.reduce_precision(x, exponent_bits=8, mantissa_bits=7)
    rest = x - hi
    mid = lax.reduce_precision(rest, exponent_bits=8, mantissa_bits=7)
    lo = lax.reduce_precision(rest - mid, exponent_bits=8, mantissa_bits=7)
    return jnp.stack([hi, mid, lo], axis=1).astype(jnp.bfloat16)


def join_three(parts):
    parts = parts.astype(jnp.float32)
    return (parts[:, 0] + parts[:, 1]) + parts[:, 2]


def local(queries, keys, values, block_list, block_count):
    row_count = queries.shape[0]
    ctx_span = keys.shape[0]
    shards = lax.axis_size("ctx")
    owners = lax.axis_size("row")
    per_owner = row_count // owners
    head_share = HEADS // shards
    share_width = head_share * HEAD_DIM
    blocks_here = ctx_span // BLOCK
    first_block = (lax.axis_index("ctx") * blocks_here).astype(jnp.int32).reshape(1)
    part, stat = local_attention(
        queries, keys, values, block_list.astype(jnp.int32), block_count.astype(jnp.int32), first_block, owners, shards
    )
    part_low = part.reshape(owners * shards, head_share * per_owner, HEAD_DIM)
    stats = jnp.transpose(stat.reshape(2, shards, head_share, owners, per_owner), (3, 1, 0, 2, 4))
    stats = stats.reshape(owners * shards, 2, head_share, per_owner)
    stats = with_layout_constraint(stats, Layout(major_to_minor=(0, 1, 2, 3)))
    stat_count = 3 * 2 * head_share * per_owner
    stat_rows = -(-stat_count // HEAD_DIM)
    stat_low = split_three(stats).reshape(owners * shards, stat_count)
    stat_low = jnp.pad(stat_low, ((0, 0), (0, stat_rows * HEAD_DIM - stat_count)))
    payload = jnp.concatenate(
        [part_low, stat_low.reshape(owners * shards, stat_rows, HEAD_DIM)], axis=1
    )
    arrived = lax.all_to_all(payload, ("row", "ctx"), 0, 0, tiled=True)
    arrived = with_layout_constraint(arrived, Layout(major_to_minor=(0, 1, 2)))
    arrived = arrived.reshape(owners, shards, head_share * per_owner + stat_rows, HEAD_DIM)
    part_in = arrived[:, :, : head_share * per_owner].reshape(owners, shards, head_share, per_owner, HEAD_DIM)
    stat_in = arrived[:, :, head_share * per_owner :].reshape(owners * shards, stat_rows * HEAD_DIM)
    stats_in = join_three(
        stat_in[:, :stat_count].reshape(owners * shards, 3, 2, head_share, per_owner)
    ).reshape(owners, shards, 2, head_share, per_owner)
    maxima = stats_in[:, :, 0]
    totals = stats_in[:, :, 1]
    row_best = jnp.max(maxima, axis=1)
    weight = jnp.exp(maxima - row_best[:, None])
    total_sum = jnp.sum(totals * weight, axis=1)
    numerator = jnp.sum(part_in.astype(jnp.float32) * weight[..., None], axis=1)
    attended = numerator / total_sum[..., None]
    attended_low = jnp.transpose(attended, (0, 2, 1, 3)).reshape(row_count, share_width)
    return attended_low.astype(jnp.bfloat16)


def solution(mesh):
    return jax.shard_map(
        local,
        mesh=mesh,
        in_specs=(P("row", None), P("ctx", None), P("ctx", None), P("row", None), P("row")),
        out_specs=P("row", "ctx"),
        check_vma=False,
    )
```

```python
import functools

import jax
import jax.numpy as jnp
from jax import lax
from jax.experimental import pallas as pl
from jax.experimental.pallas import tpu as pltpu
from jax.experimental.layout import Layout, with_layout_constraint
from jax.sharding import PartitionSpec as P

HEADS = 16
HEAD_DIM = 128
BLOCK = 128
HEADS_PER_STEP = 16


masked_fill = -1e30


def attention_kernel(shape, list_ref, count_ref, first_ref, q_ref, k_ref, v_ref, part_ref, stat_ref,
                     bias_ref, dead_ref, q_scr):
    rows, owners, per_owner, head_share, q_blocks, k_blocks, max_sel = shape

    @pl.when(pl.program_id(0) == 0)
    def _():
        first = first_ref[0]
        pos = lax.broadcasted_iota(jnp.int32, (8, rows), 1)
        q_block = ((pos % per_owner) * owners + pos // per_owner) // BLOCK
        dead = jnp.full((8, rows), jnp.inf, jnp.float32)
        biases = [jnp.full((8, rows), masked_fill, jnp.float32) for _ in range(k_blocks)]
        for a in range(q_blocks):
            for b in range(k_blocks):
                hit = jnp.int32(0)
                for slot in range(max_sel):
                    found = (list_ref[a, slot] == first + b) & (slot < count_ref[a])
                    hit = jnp.maximum(hit, jnp.where(found, 1, 0).astype(jnp.int32))
                live = (q_block == a) & (hit > 0)
                biases[b] = jnp.where(live, 0.0, biases[b])
                dead = jnp.where(live, 0.0, dead)
        for b in range(k_blocks):
            bias_ref[b * BLOCK : (b + 1) * BLOCK, :] = jnp.broadcast_to(biases[b][0:1, :], (BLOCK, rows))
        dead_ref[...] = dead

    score_scale = 1.0 / HEAD_DIM**0.5
    dead_row = dead_ref[0:1, :]
    for hl in range(head_share):
        cols = slice(hl * HEAD_DIM, (hl + 1) * HEAD_DIM)
        q_scr[...] = q_ref[:, cols].astype(jnp.float32)
        q_perm = jnp.concatenate(
            [q_scr[pl.ds(r, per_owner, stride=owners), :] for r in range(owners)], axis=0
        ).astype(jnp.bfloat16)
        scores = lax.dot_general(
            k_ref[:, cols], q_perm, (((1,), (1,)), ((), ())), preferred_element_type=jnp.float32
        )
        scores = scores * score_scale + bias_ref[...]
        seg_max = jnp.max(scores, axis=0, keepdims=True)
        probs = jnp.exp(scores - (seg_max + dead_row))
        seg_total = jnp.sum(probs, axis=0, keepdims=True)
        seg_out = lax.dot_general(
            probs.astype(jnp.bfloat16), v_ref[:, cols], (((0,), (0,)), ((), ())),
            preferred_element_type=jnp.float32,
        )
        part_ref[:, hl] = seg_out.reshape(owners, per_owner, HEAD_DIM).astype(jnp.bfloat16)
        stat_ref[0, hl : hl + 1, :] = seg_max
        stat_ref[1, hl : hl + 1, :] = seg_total


def local_attention(queries, keys, values, block_list, block_count, first_block, owners, shards):
    rows = queries.shape[0]
    per_owner = rows // owners
    ctx_span = keys.shape[0]
    step_heads = HEADS_PER_STEP
    step_width = step_heads * HEAD_DIM
    q_blocks = rows // BLOCK
    k_blocks = ctx_span // BLOCK
    max_sel = block_list.shape[1]
    shape = (rows, owners, per_owner, step_heads, q_blocks, k_blocks, max_sel)
    grid_spec = pltpu.PrefetchScalarGridSpec(
        num_scalar_prefetch=3,
        grid=(HEADS // step_heads,),
        in_specs=[
            pl.BlockSpec((rows, step_width), lambda g, *_: (0, g)),
            pl.BlockSpec((ctx_span, step_width), lambda g, *_: (0, g)),
            pl.BlockSpec((ctx_span, step_width), lambda g, *_: (0, g)),
        ],
        out_specs=[
            pl.BlockSpec((owners, step_heads, per_owner, HEAD_DIM), lambda g, *_: (0, g, 0, 0)),
            pl.BlockSpec((2, step_heads, rows), lambda g, *_: (0, g, 0)),
        ],
        scratch_shapes=[
            pltpu.VMEM((ctx_span, rows), jnp.float32),
            pltpu.VMEM((8, rows), jnp.float32),
            pltpu.VMEM((rows, HEAD_DIM), jnp.float32),
        ],
    )
    flops = 4 * HEADS * rows * ctx_span * HEAD_DIM
    return pl.pallas_call(
        functools.partial(attention_kernel, shape),
        grid_spec=grid_spec,
        out_shape=[
            jax.ShapeDtypeStruct((owners, HEADS, per_owner, HEAD_DIM), jnp.bfloat16),
            jax.ShapeDtypeStruct((2, HEADS, rows), jnp.float32),
        ],
        compiler_params=pltpu.CompilerParams(dimension_semantics=("arbitrary",)),
        cost_estimate=pl.CostEstimate(
            flops=flops,
            transcendentals=HEADS * rows * ctx_span,
            bytes_accessed=2 * (queries.size + keys.size + values.size) + 2 * rows * HEADS * HEAD_DIM,
        ),
    )(block_list, block_count, first_block, queries, keys, values)


def split_three(x):
    hi = lax.reduce_precision(x, exponent_bits=8, mantissa_bits=7)
    rest = x - hi
    mid = lax.reduce_precision(rest, exponent_bits=8, mantissa_bits=7)
    lo = lax.reduce_precision(rest - mid, exponent_bits=8, mantissa_bits=7)
    return jnp.stack([hi, mid, lo], axis=1).astype(jnp.bfloat16)


def join_three(parts):
    parts = parts.astype(jnp.float32)
    return (parts[:, 0] + parts[:, 1]) + parts[:, 2]


def local(queries, keys, values, block_list, block_count):
    row_count = queries.shape[0]
    ctx_span = keys.shape[0]
    shards = lax.axis_size("ctx")
    owners = lax.axis_size("row")
    per_owner = row_count // owners
    head_share = HEADS // shards
    share_width = head_share * HEAD_DIM
    blocks_here = ctx_span // BLOCK
    first_block = (lax.axis_index("ctx") * blocks_here).astype(jnp.int32).reshape(1)
    part, stat = local_attention(
        queries, keys, values, block_list.astype(jnp.int32), block_count.astype(jnp.int32), first_block, owners, shards
    )
    part_low = part.reshape(owners * shards, head_share * per_owner, HEAD_DIM)
    stats = jnp.transpose(stat.reshape(2, shards, head_share, owners, per_owner), (3, 1, 0, 2, 4))
    stats = stats.reshape(owners * shards, 2, head_share, per_owner)
    stats = with_layout_constraint(stats, Layout(major_to_minor=(0, 1, 2, 3)))
    stat_count = 3 * 2 * head_share * per_owner
    stat_rows = -(-stat_count // HEAD_DIM)
    stat_low = split_three(stats).reshape(owners * shards, stat_count)
    stat_low = jnp.pad(stat_low, ((0, 0), (0, stat_rows * HEAD_DIM - stat_count)))
    payload = jnp.concatenate(
        [part_low, stat_low.reshape(owners * shards, stat_rows, HEAD_DIM)], axis=1
    )
    arrived = lax.all_to_all(payload, ("row", "ctx"), 0, 0, tiled=True)
    arrived = with_layout_constraint(arrived, Layout(major_to_minor=(0, 1, 2)))
    arrived = arrived.reshape(owners, shards, head_share * per_owner + stat_rows, HEAD_DIM)
    part_in = arrived[:, :, : head_share * per_owner].reshape(owners, shards, head_share, per_owner, HEAD_DIM)
    stat_in = arrived[:, :, head_share * per_owner :].reshape(owners * shards, stat_rows * HEAD_DIM)
    stats_in = join_three(
        stat_in[:, :stat_count].reshape(owners * shards, 3, 2, head_share, per_owner)
    ).reshape(owners, shards, 2, head_share, per_owner)
    maxima = stats_in[:, :, 0]
    totals = stats_in[:, :, 1]
    row_best = jnp.max(maxima, axis=1)
    weight = jnp.exp(maxima - row_best[:, None])
    total_sum = jnp.sum(totals * weight, axis=1)
    numerator = jnp.sum(part_in.astype(jnp.float32) * weight[..., None], axis=1)
    attended = numerator / total_sum[..., None]
    attended_low = jnp.transpose(attended, (0, 2, 1, 3)).astype(jnp.bfloat16)
    attended_low = with_layout_constraint(attended_low, Layout(major_to_minor=(0, 1, 2, 3)))
    return attended_low.reshape(row_count, share_width)


def solution(mesh):
    return jax.shard_map(
        local,
        mesh=mesh,
        in_specs=(P("row", None), P("ctx", None), P("ctx", None), P("row", None), P("row")),
        out_specs=P("row", "ctx"),
        check_vma=False,
    )
```
